32 devices in a mesh: walk: 4 (over x, core), chol: 8 (over z, y).
Axes of the slice: x: 2, y: 2, z: 4, core: 2. Of those that a mesh axis runs over, the one named last changes fastest.
Arguments:
- old_walkers: bfloat16 [96, 2048, 128], P(('walk', 'chol'))
- half_chol: bfloat16 [16, 128, 2048], P('chol'), may hold values from -0.1875 to 0.1875
- parent: int32 [192], P(('walk', 'chol')), may hold values from -1 to 11, as said below
- field: float32 [192, 2048], P(('walk', 'chol')), may hold values from -0.8 to 0.8
Outputs:
- new_walkers: bfloat16 [192, 2048, 128], P(('walk', 'chol'))
- energy: float32 [192], P(('walk', 'chol'))
The draws below stay inside these ranges and needn't reach their ends.
Inputs may be any that keep to these rules, and one draw needn't show every extreme that they name: `parent`: the 4 devices that share an index of chol form a column. On each device the live slots (value >= 0) come first among its 6 slots, the rest hold -1. Each column has exactly 12 live slots, every device of it at least one, and some device of it has all 6 slots live. A live value m names the walker that the column's walk index m // 3 holds as its local walker m % 3.
All inputs are finite; a program needn't handle non-finite values.
Results may differ from the reference program's by a relative error of at most 0.0062.
Values may be sent and summed in bfloat16 or wider, within the bound.
No kernel may reach another device: no remote copies, remote signals or barrier semaphores. Data moves between devices by JAX's collectives and lax.ppermute only.
A program may use at most 192 MiB of HBM per device.

```python
import math
import jax
import jax.numpy as jnp
from jax import lax

NORB = 2048
NELEC = 128
OLD_DEV = 3
ITERS = 3
SLOT_DEV = 6
NCHOL = 16
OLD = 96
SLOTS = 192
N_WALK = 4
N_CHOL = 8


def draw_old_walkers(key, part):
    key_diag, key_rest = jax.random.split(key)
    diagonal = jax.random.uniform(key_diag, (OLD, 1, NELEC), jnp.float32, 1.0, 1.5)
    entries = jax.random.normal(key_rest, (OLD, NORB, NELEC), jnp.float32)
    orbital = lax.broadcasted_iota(jnp.int32, (1, NORB, NELEC), 1)
    electron = lax.broadcasted_iota(jnp.int32, (1, NORB, NELEC), 2)
    scales = jnp.where(orbital < NELEC, 0.28 / math.sqrt(NELEC), 1.0 / math.sqrt(NORB))
    walkers = jnp.where(orbital == electron, diagonal, scales * entries)
    return walkers.astype(jnp.bfloat16)


def column_parents(key):
    key_full, key_units, key_parent = jax.random.split(key, 3)
    full_device = jax.random.randint(key_full, (), 0, N_WALK)
    extra_count = OLD_DEV * (N_WALK - 2) - (N_WALK - 1)
    shuffled = jax.random.permutation(key_units, (N_WALK - 1) * (SLOT_DEV - 1))
    chosen = (shuffled < extra_count).astype(jnp.int32).reshape(N_WALK - 1, SLOT_DEV - 1)
    others = 1 + jnp.sum(chosen, axis=1)
    walk_index = jnp.arange(N_WALK, dtype=jnp.int32)
    position = jnp.clip(walk_index - (walk_index > full_device).astype(jnp.int32), 0, N_WALK - 2)
    counts = jnp.where(walk_index == full_device, SLOT_DEV, others[position])
    parents = jax.random.randint(key_parent, (N_WALK, SLOT_DEV), 0, OLD_DEV * N_WALK)
    parents = parents.at[0, 0].set(OLD_DEV * N_WALK - 1)
    living = jnp.arange(SLOT_DEV, dtype=jnp.int32)[None, :] < counts[:, None]
    return jnp.where(living, parents, -1)


def column_key(key, column):
    return jax.random.fold_in(key, column)


def draw_parent(key, part):
    column_keys = jax.vmap(column_key, in_axes=(None, 0))(key, jnp.arange(N_CHOL, dtype=jnp.int32))
    tables = jax.vmap(column_parents)(column_keys)
    return jnp.transpose(tables, (1, 0, 2)).reshape(SLOTS).astype(jnp.int32)


def shard_levels(own_key, shape, pieces, least, largest):
    def one(dim, shards_of):
        draws = jax.random.uniform(jax.random.fold_in(jax.random.fold_in(own_key, 6), dim), (shards_of,), jnp.float32, least / len(pieces), largest / len(pieces))
        return jnp.repeat(jnp.exp(draws), shape[dim] // shards_of).reshape((-1,) + (1,) * (len(shape) - dim - 1))

    level = one(*pieces[0])
    for cut in pieces[1:]:
        level = level * one(*cut)
    return level


def bell_draw(stream_key, dims, scale, most, pieces=(), held_as=jnp.bfloat16):
    factor_of = shard_levels(stream_key, dims, pieces, -0.22, 0.18) if pieces else 1.0
    drawn = jax.random.normal(stream_key, dims, jnp.float32) * scale * factor_of
    return jnp.minimum(jnp.maximum(drawn, -most), most).astype(held_as)


def setup_inputs(seed: int = 0) -> dict:
    splits = jax.random.split(jax.random.key(seed), 5)
    old_walkers = draw_old_walkers(jax.random.fold_in(splits[4], 71), 0)
    half_chol = bell_draw(splits[1], (NCHOL, NELEC, NORB), (NELEC * NCHOL // 2) ** -0.5, 0.1875, ((0, 8),))
    parent = draw_parent(jax.random.fold_in(splits[4], 71), 0)
    field = bell_draw(splits[3], (SLOTS, NORB), 0.2, 0.8, ((0, 32),), jnp.float32)
    return {"old_walkers": old_walkers, "half_chol": half_chol, "parent": parent, "field": field}


def newton_theta(walker):
    intersection = walker[:NELEC, :]
    identity = jnp.eye(NELEC, dtype=jnp.float32)
    inverse = identity / jnp.diagonal(intersection)[None, :]
    for sweep in range(ITERS):
        step_term = 2.0 * identity - jnp.dot(intersection, inverse, precision=lax.Precision.HIGHEST)
        inverse = jnp.dot(inverse, step_term, precision=lax.Precision.HIGHEST)
    theta = jnp.dot(walker, inverse, precision=lax.Precision.HIGHEST)
    return theta.astype(jnp.bfloat16)


def walker_energy(theta, chol_wide):
    blocks = jnp.einsum("gin,nj->gij", chol_wide, theta.astype(jnp.float32), precision=lax.Precision.HIGHEST)
    traces = jnp.trace(blocks, axis1=1, axis2=2)
    crossed = jnp.sum(blocks * jnp.swapaxes(blocks, 1, 2), axis=(1, 2))
    return 0.5 * jnp.sum(traces * traces - crossed)


def reference(old_walkers, half_chol, parent, field):
    slot_index = jnp.arange(SLOTS, dtype=jnp.int32)
    column_index = (slot_index // SLOT_DEV) % N_CHOL
    living = parent >= 0
    parent_index = jnp.maximum(parent, 0)
    source = ((parent_index // OLD_DEV) * N_CHOL + column_index) * OLD_DEV + parent_index % OLD_DEV
    kicked = (jnp.exp(field)[:, :, None] * old_walkers[source].astype(jnp.float32)).astype(jnp.bfloat16)
    new_walkers = jnp.where(living[:, None, None], kicked, jnp.zeros_like(kicked))
    chol_wide = half_chol.astype(jnp.float32)
    live_slots = jnp.nonzero(living, size=OLD)[0].astype(jnp.int32)

    def one_slot(position):
        walker = kicked[position].astype(jnp.float32)
        return walker_energy(newton_theta(walker), chol_wide)

    values = lax.map(one_slot, live_slots)
    energy = jnp.zeros((SLOTS,), jnp.float32).at[live_slots].set(values)
    return new_walkers, energy
```

```python
import jax
import jax.numpy as jnp
from jax import lax
from jax.sharding import PartitionSpec as P

ITERS = 3


def green_half(walkers):
    widened = walkers.astype(jnp.float32)
    electrons = walkers.shape[2]
    intersection = widened[:, :electrons, :]
    identity = jnp.eye(electrons, dtype=jnp.float32)
    diagonal = jnp.diagonal(intersection, axis1=1, axis2=2)
    inverse = identity[None, :, :] / diagonal[:, None, :]
    for sweep in range(ITERS):
        product = jnp.einsum("wij,wjk->wik", intersection, inverse, precision=lax.Precision.HIGHEST)
        inverse = jnp.einsum(
            "wij,wjk->wik",
            inverse,
            2.0 * identity[None, :, :] - product,
            precision=lax.Precision.HIGHEST,
        )
    theta = jnp.einsum("wnk,wkj->wnj", widened, inverse, precision=lax.Precision.HIGHEST)
    return theta.astype(jnp.bfloat16)


def block_energy(theta, vectors):
    blocks = jnp.einsum("gin,wnj->wgij", vectors, theta, preferred_element_type=jnp.float32)
    traces = jnp.einsum("wgii->wg", blocks)
    crossed = jnp.sum(blocks * jnp.swapaxes(blocks, 2, 3), axis=(2, 3))
    return 0.5 * jnp.sum(traces * traces - crossed, axis=1)


def swap_pairs(x, axis, size, bit):
    perm = [(i, i ^ bit) for i in range(size)]
    return lax.ppermute(x, axis, perm)


def body(old_walkers, half_chol, parent, field):
    n_walk = lax.axis_size("walk")
    old_dev = old_walkers.shape[0]
    slot_dev = parent.shape[0]
    walk_id = lax.axis_index("walk")
    core = walk_id % 2

    local_g = half_chol.shape[0]
    half_g = local_g // 2
    mine = lax.dynamic_slice_in_dim(half_chol, core * half_g, half_g, axis=0)
    gathered = lax.all_gather(mine, "chol", axis=0, tiled=True)
    other = swap_pairs(gathered, "walk", n_walk, 1)

    across = swap_pairs(old_walkers, "walk", n_walk, 2)
    beside = swap_pairs(old_walkers, "walk", n_walk, 1)
    diagonal_peer = swap_pairs(across, "walk", n_walk, 1)
    column = jnp.concatenate([old_walkers, beside, across, diagonal_peer], axis=0)

    living = parent >= 0
    source = jnp.maximum(parent, 0)
    relative = (source // old_dev) ^ walk_id
    index = relative * old_dev + source % old_dev
    kicked = (jnp.exp(field)[:, :, None] * column[index].astype(jnp.float32)).astype(jnp.bfloat16)
    new_walkers = jnp.where(living[:, None, None], kicked, jnp.zeros_like(kicked))
    theta = green_half(kicked)
    energy = block_energy(theta, gathered) + block_energy(theta, other)
    energy = jnp.where(living, energy, 0.0)
    return (new_walkers, energy)


def solution(mesh):
    return jax.shard_map(
        body,
        mesh=mesh,
        in_specs=(
            P(("walk", "chol"), None, None),
            P("chol", None, None),
            P(("walk", "chol")),
            P(("walk", "chol"), None),
        ),
        out_specs=(P(("walk", "chol"), None, None), P(("walk", "chol"))),
        check_vma=False,
    )
```

```python
import jax
import jax.numpy as jnp
from jax import lax
from jax.sharding import PartitionSpec as P

ITERS = 3


def green_half(walkers):
    widened = walkers.astype(jnp.float32)
    electrons = walkers.shape[2]
    intersection = widened[:, :electrons, :]
    identity = jnp.eye(electrons, dtype=jnp.float32)
    diagonal = jnp.diagonal(intersection, axis1=1, axis2=2)
    inverse = identity[None, :, :] / diagonal[:, None, :]
    for sweep in range(ITERS):
        product = jnp.einsum("wij,wjk->wik", intersection, inverse, precision=lax.Precision.HIGHEST)
        inverse = jnp.einsum(
            "wij,wjk->wik",
            inverse,
            2.0 * identity[None, :, :] - product,
            precision=lax.Precision.HIGHEST,
        )
    theta = jnp.einsum("wnk,wkj->wnj", widened, inverse, precision=lax.Precision.HIGHEST)
    return theta.astype(jnp.bfloat16)


def block_energy(theta, vectors):
    blocks = jnp.einsum("gin,wnj->wgij", vectors, theta, preferred_element_type=jnp.float32)
    traces = jnp.einsum("wgii->wg", blocks)
    crossed = jnp.sum(blocks * jnp.swapaxes(blocks, 2, 3), axis=(2, 3))
    return 0.5 * jnp.sum(traces * traces - crossed, axis=1)


def swap_pairs(x, axis, size, bit):
    perm = [(i, i ^ bit) for i in range(size)]
    return lax.ppermute(x, axis, perm)


def body(old_walkers, half_chol, parent, field):
    n_walk = lax.axis_size("walk")
    old_dev = old_walkers.shape[0]
    slot_dev = parent.shape[0]
    walk_id = lax.axis_index("walk")
    core = walk_id % 2

    local_g = half_chol.shape[0]
    half_g = local_g // 2
    mine = lax.dynamic_slice_in_dim(half_chol, core * half_g, half_g, axis=0)
    n_chol = lax.axis_size("chol")
    order = list(range(0, n_chol, 2)) + list(range(n_chol - 1, 0, -2))
    forward = [(order[i], order[(i + 1) % n_chol]) for i in range(n_chol)]
    backward = [(b, a) for a, b in forward]
    n_forward = n_chol // 2
    pieces = []
    current = mine
    for step in range(n_forward):
        current = lax.ppermute(current, "chol", forward)
        pieces.append(current)
    current = mine
    for step in range(n_chol - 1 - n_forward):
        current = lax.ppermute(current, "chol", backward)
        pieces.append(current)
    handed = [swap_pairs(piece, "walk", n_walk, 1) for piece in pieces]
    vectors = jnp.concatenate([half_chol] + pieces + handed, axis=0)

    across = swap_pairs(old_walkers, "walk", n_walk, 2)
    beside = swap_pairs(old_walkers, "walk", n_walk, 1)
    diagonal_peer = swap_pairs(across, "walk", n_walk, 1)
    column = jnp.concatenate([old_walkers, beside, across, diagonal_peer], axis=0)

    living = parent >= 0
    source = jnp.maximum(parent, 0)
    relative = (source // old_dev) ^ walk_id
    index = relative * old_dev + source % old_dev
    kicked = (jnp.exp(field)[:, :, None] * column[index].astype(jnp.float32)).astype(jnp.bfloat16)
    new_walkers = jnp.where(living[:, None, None], kicked, jnp.zeros_like(kicked))
    theta = green_half(kicked)
    energy = block_energy(theta, vectors)
    energy = jnp.where(living, energy, 0.0)
    return (new_walkers, energy)


def solution(mesh):
    return jax.shard_map(
        body,
        mesh=mesh,
        in_specs=(
            P(("walk", "chol"), None, None),
            P("chol", None, None),
            P(("walk", "chol")),
            P(("walk", "chol"), None),
        ),
        out_specs=(P(("walk", "chol"), None, None), P(("walk", "chol"))),
        check_vma=False,
    )
```

```python
import jax
import jax.numpy as jnp
from jax import lax
from jax.sharding import PartitionSpec as P

ITERS = 3


def green_half(walkers):
    widened = walkers.astype(jnp.float32)
    electrons = walkers.shape[2]
    intersection = widened[:, :electrons, :]
    identity = jnp.eye(electrons, dtype=jnp.float32)
    diagonal = jnp.diagonal(intersection, axis1=1, axis2=2)
    inverse = identity[None, :, :] / diagonal[:, None, :]
    for sweep in range(ITERS):
        product = jnp.einsum("wij,wjk->wik", intersection, inverse, precision=lax.Precision.HIGHEST)
        inverse = jnp.einsum(
            "wij,wjk->wik",
            inverse,
            2.0 * identity[None, :, :] - product,
            precision=lax.Precision.HIGHEST,
        )
    theta = jnp.einsum("wnk,wkj->wnj", widened, inverse, precision=lax.Precision.HIGHEST)
    return theta.astype(jnp.bfloat16)


def block_energy(theta, vectors):
    blocks = jnp.einsum("gin,wnj->wgij", vectors, theta, preferred_element_type=jnp.float32)
    traces = jnp.einsum("wgii->wg", blocks)
    crossed = jnp.sum(blocks * jnp.swapaxes(blocks, 2, 3), axis=(2, 3))
    return 0.5 * jnp.sum(traces * traces - crossed, axis=1)


def swap_pairs(x, axis, size, bit):
    perm = [(i, i ^ bit) for i in range(size)]
    return lax.ppermute(x, axis, perm)


def body(old_walkers, half_chol, parent, field):
    n_walk = lax.axis_size("walk")
    old_dev = old_walkers.shape[0]
    slot_dev = parent.shape[0]
    walk_id = lax.axis_index("walk")
    core = walk_id % 2

    across = swap_pairs(old_walkers, "walk", n_walk, 2)
    beside = swap_pairs(old_walkers, "walk", n_walk, 1)
    diagonal_peer = swap_pairs(across, "walk", n_walk, 1)
    local_g = half_chol.shape[0]
    half_g = local_g // 2
    mine = lax.dynamic_slice_in_dim(half_chol, core * half_g, half_g, axis=0)
    n_chol = lax.axis_size("chol")
    order = list(range(0, n_chol, 2)) + list(range(n_chol - 1, 0, -2))
    forward = [(order[i], order[(i + 1) % n_chol]) for i in range(n_chol)]
    backward = [(b, a) for a, b in forward]
    n_forward = n_chol // 2
    n_backward = n_chol - 1 - n_forward
    pieces = []
    ahead = mine
    behind = mine
    for step in range(n_forward):
        ahead = lax.ppermute(ahead, "chol", forward)
        if step < n_backward:
            behind = lax.ppermute(behind, "chol", backward)
            ahead, behind = lax.optimization_barrier((ahead, behind))
            pieces.append(behind)
        pieces.append(ahead)
    handed = [swap_pairs(piece, "walk", n_walk, 1) for piece in pieces]
    vectors = jnp.concatenate([half_chol] + pieces + handed, axis=0)

    column = jnp.concatenate([old_walkers, beside, across, diagonal_peer], axis=0)

    living = parent >= 0
    source = jnp.maximum(parent, 0)
    relative = (source // old_dev) ^ walk_id
    index = relative * old_dev + source % old_dev
    kicked = (jnp.exp(field)[:, :, None] * column[index].astype(jnp.float32)).astype(jnp.bfloat16)
    new_walkers = jnp.where(living[:, None, None], kicked, jnp.zeros_like(kicked))
    theta = green_half(kicked)
    energy = block_energy(theta, vectors)
    energy = jnp.where(living, energy, 0.0)
    return (new_walkers, energy)


def solution(mesh):
    return jax.shard_map(
        body,
        mesh=mesh,
        in_specs=(
            P(("walk", "chol"), None, None),
            P("chol", None, None),
            P(("walk", "chol")),
            P(("walk", "chol"), None),
        ),
        out_specs=(P(("walk", "chol"), None, None), P(("walk", "chol"))),
        check_vma=False,
    )
```

```python
import jax
import jax.numpy as jnp
from jax import lax
from jax.sharding import PartitionSpec as P

ITERS = 3


def green_half(walkers):
    widened = walkers.astype(jnp.float32)
    electrons = walkers.shape[2]
    intersection = widened[:, :electrons, :]
    identity = jnp.eye(electrons, dtype=jnp.float32)
    diagonal = jnp.diagonal(intersection, axis1=1, axis2=2)
    inverse = identity[None, :, :] / diagonal[:, None, :]
    for sweep in range(ITERS):
        product = jnp.einsum("wij,wjk->wik", intersection, inverse, precision=lax.Precision.HIGHEST)
        inverse = jnp.einsum(
            "wij,wjk->wik",
            inverse,
            2.0 * identity[None, :, :] - product,
            precision=lax.Precision.HIGHEST,
        )
    theta = jnp.einsum("wnk,wkj->wnj", widened, inverse, precision=lax.Precision.HIGHEST)
    return theta.astype(jnp.bfloat16)


def block_energy(theta, vectors):
    blocks = jnp.einsum("gin,wnj->wgij", vectors, theta, preferred_element_type=jnp.float32)
    traces = jnp.einsum("wgii->wg", blocks)
    crossed = jnp.sum(blocks * jnp.swapaxes(blocks, 2, 3), axis=(2, 3))
    return 0.5 * jnp.sum(traces * traces - crossed, axis=1)


def swap_pairs(x, axis, size, bit):
    perm = [(i, i ^ bit) for i in range(size)]
    return lax.ppermute(x, axis, perm)


def kick(old_walkers, beside, across, diagonal_peer, parent, field, walk_id):
    old_dev = old_walkers.shape[0]
    column = jnp.concatenate([old_walkers, beside, across, diagonal_peer], axis=0)
    living = parent >= 0
    source = jnp.maximum(parent, 0)
    relative = (source // old_dev) ^ walk_id
    index = relative * old_dev + source % old_dev
    kicked = (jnp.exp(field)[:, :, None] * column[index].astype(jnp.float32)).astype(jnp.bfloat16)
    new_walkers = jnp.where(living[:, None, None], kicked, jnp.zeros_like(kicked))
    return new_walkers, green_half(kicked)


def body(old_walkers, half_chol, parent, field):
    n_walk = lax.axis_size("walk")
    walk_id = lax.axis_index("walk")
    core = walk_id % 2

    across = swap_pairs(old_walkers, "walk", n_walk, 2)
    beside = swap_pairs(old_walkers, "walk", n_walk, 1)

    local_g = half_chol.shape[0]
    half_g = local_g // 2
    mine = lax.dynamic_slice_in_dim(half_chol, core * half_g, half_g, axis=0)
    n_chol = lax.axis_size("chol")
    order = list(range(0, n_chol, 2)) + list(range(n_chol - 1, 0, -2))
    forward = [(order[i], order[(i + 1) % n_chol]) for i in range(n_chol)]
    backward = [(b, a) for a, b in forward]
    n_forward = n_chol // 2
    n_backward = n_chol - 1 - n_forward
    walker_step = max(n_forward - 2, 0)
    pieces = []
    handed = []
    ahead = mine
    behind = mine
    new_walkers = theta = None
    for step in range(n_forward):
        ahead = lax.ppermute(ahead, "chol", forward)
        carried = [ahead]
        if step < n_backward:
            behind = lax.ppermute(behind, "chol", backward)
            carried.append(behind)
        if step == walker_step:
            carried += [across, beside]
        if step == n_forward - 1:
            diagonal_peer = swap_pairs(across, "walk", n_walk, 1)
            new_walkers, theta = kick(old_walkers, beside, across, diagonal_peer, parent, field, walk_id)
            carried += [new_walkers, theta]
        carried = list(lax.optimization_barrier(tuple(carried)))
        ahead = carried.pop(0)
        arrived = [ahead]
        if step < n_backward:
            behind = carried.pop(0)
            arrived.append(behind)
        if step == walker_step:
            across, beside = carried.pop(0), carried.pop(0)
        if step == n_forward - 1:
            new_walkers, theta = carried.pop(0), carried.pop(0)
        for piece in arrived:
            pieces.append(piece)
            handed.append(swap_pairs(piece, "walk", n_walk, 1))
    if theta is None:
        diagonal_peer = swap_pairs(across, "walk", n_walk, 1)
        new_walkers, theta = kick(old_walkers, beside, across, diagonal_peer, parent, field, walk_id)
    vectors = jnp.concatenate([half_chol] + pieces + handed, axis=0)

    living = parent >= 0
    energy = block_energy(theta, vectors)
    energy = jnp.where(living, energy, 0.0)
    return (new_walkers, energy)


def solution(mesh):
    return jax.shard_map(
        body,
        mesh=mesh,
        in_specs=(
            P(("walk", "chol"), None, None),
            P("chol", None, None),
            P(("walk", "chol")),
            P(("walk", "chol"), None),
        ),
        out_specs=(P(("walk", "chol"), None, None), P(("walk", "chol"))),
        check_vma=False,
    )
```

```python
import jax
import jax.numpy as jnp
from jax import lax
from jax.sharding import PartitionSpec as P
from jax.experimental import pallas as pl
from jax.experimental.pallas import tpu as pltpu

ITERS = 3


def green_half(walkers):
    widened = walkers.astype(jnp.float32)
    electrons = walkers.shape[2]
    intersection = widened[:, :electrons, :]
    identity = jnp.eye(electrons, dtype=jnp.float32)
    diagonal = jnp.diagonal(intersection, axis1=1, axis2=2)
    inverse = identity[None, :, :] / diagonal[:, None, :]
    for sweep in range(ITERS):
        product = jnp.einsum("wij,wjk->wik", intersection, inverse, precision=lax.Precision.HIGHEST)
        inverse = jnp.einsum(
            "wij,wjk->wik",
            inverse,
            2.0 * identity[None, :, :] - product,
            precision=lax.Precision.HIGHEST,
        )
    theta = jnp.einsum("wnk,wkj->wnj", widened, inverse, precision=lax.Precision.HIGHEST)
    return theta.astype(jnp.bfloat16)


def energy_kernel(*refs):
    theta_ref = refs[0]
    chol_refs = refs[1:-1]
    out_ref = refs[-1]
    n_slot, _, electrons = theta_ref.shape
    rows = lax.broadcasted_iota(jnp.int32, (electrons, electrons), 0)
    cols = lax.broadcasted_iota(jnp.int32, (electrons, electrons), 1)
    diagonal = rows == cols
    out_ref[...] = jnp.zeros(out_ref.shape, jnp.float32)
    for chol_ref in chol_refs:
        def per_vector(g, carry, chol_ref=chol_ref):
            vector = chol_ref[g]

            def per_slot(s, inner):
                blocks = jnp.dot(vector, theta_ref[s], preferred_element_type=jnp.float32)
                trace = jnp.sum(jnp.where(diagonal, blocks, 0.0), keepdims=True)
                crossed = jnp.sum(blocks * blocks.T, keepdims=True)
                value = 0.5 * (trace * trace - crossed)
                out_ref[pl.ds(s, 1), :] += jnp.broadcast_to(value, (1, out_ref.shape[1]))
                return inner

            return lax.fori_loop(0, n_slot, per_slot, carry)

        lax.fori_loop(0, chol_ref.shape[0], per_vector, 0)


def block_energy(theta, pieces):
    n_slot = theta.shape[0]
    vmem = pltpu.MemorySpace.VMEM
    held = sum(p.size * p.dtype.itemsize for p in pieces) + theta.size * theta.dtype.itemsize
    out = pl.pallas_call(
        energy_kernel,
        out_shape=jax.ShapeDtypeStruct((n_slot, 128), jnp.float32),
        in_specs=[pl.BlockSpec(memory_space=vmem)] * (1 + len(pieces)),
        out_specs=pl.BlockSpec(memory_space=vmem),
        compiler_params=pltpu.CompilerParams(vmem_limit_bytes=int(held + (16 << 20))),
    )(theta, *pieces)
    return out[:, 0]


def swap_pairs(x, axis, size, bit):
    perm = [(i, i ^ bit) for i in range(size)]
    return lax.ppermute(x, axis, perm)


def kick(old_walkers, beside, across, diagonal_peer, parent, field, walk_id):
    old_dev = old_walkers.shape[0]
    column = jnp.concatenate([old_walkers, beside, across, diagonal_peer], axis=0)
    living = parent >= 0
    source = jnp.maximum(parent, 0)
    relative = (source // old_dev) ^ walk_id
    index = relative * old_dev + source % old_dev
    kicked = (jnp.exp(field)[:, :, None] * column[index].astype(jnp.float32)).astype(jnp.bfloat16)
    new_walkers = jnp.where(living[:, None, None], kicked, jnp.zeros_like(kicked))
    return new_walkers, green_half(kicked)


def body(old_walkers, half_chol, parent, field):
    n_walk = lax.axis_size("walk")
    walk_id = lax.axis_index("walk")
    core = walk_id % 2

    across = swap_pairs(old_walkers, "walk", n_walk, 2)
    beside = swap_pairs(old_walkers, "walk", n_walk, 1)

    local_g = half_chol.shape[0]
    half_g = local_g // 2
    mine = lax.dynamic_slice_in_dim(half_chol, core * half_g, half_g, axis=0)
    n_chol = lax.axis_size("chol")
    order = list(range(0, n_chol, 2)) + list(range(n_chol - 1, 0, -2))
    forward = [(order[i], order[(i + 1) % n_chol]) for i in range(n_chol)]
    backward = [(b, a) for a, b in forward]
    n_forward = n_chol // 2
    n_backward = n_chol - 1 - n_forward
    walker_step = max(n_forward - 2, 0)
    pieces = []
    handed = []
    ahead = mine
    behind = mine
    new_walkers = theta = None
    for step in range(n_forward):
        ahead = lax.ppermute(ahead, "chol", forward)
        carried = [ahead]
        if step < n_backward:
            behind = lax.ppermute(behind, "chol", backward)
            carried.append(behind)
        if step == walker_step:
            carried += [across, beside]
        if step == n_forward - 1:
            diagonal_peer = swap_pairs(across, "walk", n_walk, 1)
            new_walkers, theta = kick(old_walkers, beside, across, diagonal_peer, parent, field, walk_id)
            carried += [new_walkers, theta]
        carried = list(lax.optimization_barrier(tuple(carried)))
        ahead = carried.pop(0)
        arrived = [ahead]
        if step < n_backward:
            behind = carried.pop(0)
            arrived.append(behind)
        if step == walker_step:
            across, beside = carried.pop(0), carried.pop(0)
        if step == n_forward - 1:
            new_walkers, theta = carried.pop(0), carried.pop(0)
        for piece in arrived:
            pieces.append(piece)
            handed.append(swap_pairs(piece, "walk", n_walk, 1))
    if theta is None:
        diagonal_peer = swap_pairs(across, "walk", n_walk, 1)
        new_walkers, theta = kick(old_walkers, beside, across, diagonal_peer, parent, field, walk_id)

    living = parent >= 0
    energy = block_energy(theta, [half_chol] + pieces + handed)
    energy = jnp.where(living, energy, 0.0)
    return (new_walkers, energy)


def solution(mesh):
    return jax.shard_map(
        body,
        mesh=mesh,
        in_specs=(
            P(("walk", "chol"), None, None),
            P("chol", None, None),
            P(("walk", "chol")),
            P(("walk", "chol"), None),
        ),
        out_specs=(P(("walk", "chol"), None, None), P(("walk", "chol"))),
        check_vma=False,
    )
```

```python
import jax
import jax.numpy as jnp
from jax import lax
from jax.sharding import PartitionSpec as P
from jax.experimental import pallas as pl
from jax.experimental.pallas import tpu as pltpu

ITERS = 3


def green_half(walkers):
    widened = walkers.astype(jnp.float32)
    electrons = walkers.shape[2]
    intersection = widened[:, :electrons, :]
    identity = jnp.eye(electrons, dtype=jnp.float32)
    diagonal = jnp.diagonal(intersection, axis1=1, axis2=2)
    inverse = identity[None, :, :] / diagonal[:, None, :]
    for sweep in range(ITERS):
        product = jnp.einsum("wij,wjk->wik", intersection, inverse, precision=lax.Precision.HIGHEST)
        inverse = jnp.einsum(
            "wij,wjk->wik",
            inverse,
            2.0 * identity[None, :, :] - product,
            precision=lax.Precision.HIGHEST,
        )
    theta = jnp.einsum("wnk,wkj->wnj", widened, inverse, precision=lax.Precision.HIGHEST)
    return theta.astype(jnp.bfloat16)


def energy_kernel(*refs):
    theta_ref = refs[0]
    chol_refs = refs[1:-3]
    out_ref, crossed_ref, square_ref = refs[-3:]
    n_slot, _, electrons = theta_ref.shape
    lanes = out_ref.shape[1]
    rows = lax.broadcasted_iota(jnp.int32, (electrons, electrons), 0)
    cols = lax.broadcasted_iota(jnp.int32, (electrons, electrons), 1)
    diagonal = rows == cols
    crossed_ref[...] = jnp.zeros(crossed_ref.shape, jnp.float32)
    square_ref[...] = jnp.zeros(square_ref.shape, jnp.float32)
    for chol_ref in chol_refs:
        def per_vector(g, carry, chol_ref=chol_ref):
            vector = chol_ref[g]
            for s in range(n_slot):
                blocks = jnp.dot(vector, theta_ref[s], preferred_element_type=jnp.float32)
                crossed_ref[s] += blocks * blocks.T
                diag = jnp.sum(jnp.where(diagonal, blocks, 0.0), axis=0, keepdims=True)
                trace = jnp.sum(diag, axis=1, keepdims=True)
                square_ref[pl.ds(s, 1), :] += jnp.broadcast_to(trace * trace, (1, lanes))
            return carry

        lax.fori_loop(0, chol_ref.shape[0], per_vector, 0)
    for s in range(n_slot):
        crossed = jnp.sum(crossed_ref[s], keepdims=True)
        out_ref[pl.ds(s, 1), :] = 0.5 * (square_ref[pl.ds(s, 1), :] - jnp.broadcast_to(crossed, (1, lanes)))


def block_energy(theta, pieces):
    n_slot, _, electrons = theta.shape
    vmem = pltpu.MemorySpace.VMEM
    held = sum(p.size * p.dtype.itemsize for p in pieces) + theta.size * theta.dtype.itemsize
    out = pl.pallas_call(
        energy_kernel,
        out_shape=jax.ShapeDtypeStruct((n_slot, 128), jnp.float32),
        in_specs=[pl.BlockSpec(memory_space=vmem)] * (1 + len(pieces)),
        out_specs=pl.BlockSpec(memory_space=vmem),
        scratch_shapes=[
            pltpu.VMEM((n_slot, electrons, electrons), jnp.float32),
            pltpu.VMEM((n_slot, 128), jnp.float32),
        ],
        compiler_params=pltpu.CompilerParams(vmem_limit_bytes=int(held + (16 << 20))),
    )(theta, *pieces)
    return out[:, 0]


def swap_pairs(x, axis, size, bit):
    perm = [(i, i ^ bit) for i in range(size)]
    return lax.ppermute(x, axis, perm)


def kick(old_walkers, beside, across, diagonal_peer, parent, field, walk_id):
    old_dev = old_walkers.shape[0]
    column = jnp.concatenate([old_walkers, beside, across, diagonal_peer], axis=0)
    living = parent >= 0
    source = jnp.maximum(parent, 0)
    relative = (source // old_dev) ^ walk_id
    index = relative * old_dev + source % old_dev
    kicked = (jnp.exp(field)[:, :, None] * column[index].astype(jnp.float32)).astype(jnp.bfloat16)
    new_walkers = jnp.where(living[:, None, None], kicked, jnp.zeros_like(kicked))
    return new_walkers, green_half(kicked)


def body(old_walkers, half_chol, parent, field):
    n_walk = lax.axis_size("walk")
    walk_id = lax.axis_index("walk")
    core = walk_id % 2

    across = swap_pairs(old_walkers, "walk", n_walk, 2)
    beside = swap_pairs(old_walkers, "walk", n_walk, 1)

    local_g = half_chol.shape[0]
    half_g = local_g // 2
    mine = lax.dynamic_slice_in_dim(half_chol, core * half_g, half_g, axis=0)
    n_chol = lax.axis_size("chol")
    order = list(range(0, n_chol, 2)) + list(range(n_chol - 1, 0, -2))
    forward = [(order[i], order[(i + 1) % n_chol]) for i in range(n_chol)]
    backward = [(b, a) for a, b in forward]
    n_forward = n_chol // 2
    n_backward = n_chol - 1 - n_forward
    walker_step = max(n_forward - 2, 0)
    pieces = []
    handed = []
    ahead = mine
    behind = mine
    new_walkers = theta = None
    for step in range(n_forward):
        ahead = lax.ppermute(ahead, "chol", forward)
        carried = [ahead]
        if step < n_backward:
            behind = lax.ppermute(behind, "chol", backward)
            carried.append(behind)
        if step == walker_step:
            carried += [across, beside]
        if step == n_forward - 1:
            diagonal_peer = swap_pairs(across, "walk", n_walk, 1)
            new_walkers, theta = kick(old_walkers, beside, across, diagonal_peer, parent, field, walk_id)
            carried += [new_walkers, theta]
        carried = list(lax.optimization_barrier(tuple(carried)))
        ahead = carried.pop(0)
        arrived = [ahead]
        if step < n_backward:
            behind = carried.pop(0)
            arrived.append(behind)
        if step == walker_step:
            across, beside = carried.pop(0), carried.pop(0)
        if step == n_forward - 1:
            new_walkers, theta = carried.pop(0), carried.pop(0)
        for piece in arrived:
            pieces.append(piece)
            handed.append(swap_pairs(piece, "walk", n_walk, 1))
    if theta is None:
        diagonal_peer = swap_pairs(across, "walk", n_walk, 1)
        new_walkers, theta = kick(old_walkers, beside, across, diagonal_peer, parent, field, walk_id)

    living = parent >= 0
    energy = block_energy(theta, [half_chol] + pieces + handed)
    energy = jnp.where(living, energy, 0.0)
    return (new_walkers, energy)


def solution(mesh):
    return jax.shard_map(
        body,
        mesh=mesh,
        in_specs=(
            P(("walk", "chol"), None, None),
            P("chol", None, None),
            P(("walk", "chol")),
            P(("walk", "chol"), None),
        ),
        out_specs=(P(("walk", "chol"), None, None), P(("walk", "chol"))),
        check_vma=False,
    )
```

```python
import jax
import jax.numpy as jnp
from jax import lax
from jax.sharding import PartitionSpec as P
from jax.experimental import pallas as pl
from jax.experimental.pallas import tpu as pltpu

ITERS = 3


def green_half(walkers):
    widened = walkers.astype(jnp.float32)
    electrons = walkers.shape[2]
    intersection = widened[:, :electrons, :]
    identity = jnp.eye(electrons, dtype=jnp.float32)
    diagonal = jnp.diagonal(intersection, axis1=1, axis2=2)
    inverse = identity[None, :, :] / diagonal[:, None, :]
    for sweep in range(ITERS):
        product = jnp.einsum("wij,wjk->wik", intersection, inverse, precision=lax.Precision.HIGHEST)
        inverse = jnp.einsum(
            "wij,wjk->wik",
            inverse,
            2.0 * identity[None, :, :] - product,
            precision=lax.Precision.HIGHEST,
        )
    theta = jnp.einsum("wnk,wkj->wnj", widened, inverse, precision=lax.Precision.HIGHEST)
    return theta.astype(jnp.bfloat16)


def energy_kernel(*refs):
    theta_ref = refs[0]
    chol_refs = refs[1:-3]
    out_ref, crossed_ref, square_ref = refs[-3:]
    n_slot, _, electrons = theta_ref.shape
    lanes = out_ref.shape[1]
    rows = lax.broadcasted_iota(jnp.int32, (electrons, electrons), 0)
    cols = lax.broadcasted_iota(jnp.int32, (electrons, electrons), 1)
    diagonal = rows == cols
    crossed_ref[...] = jnp.zeros(crossed_ref.shape, jnp.float32)
    square_ref[...] = jnp.zeros(square_ref.shape, jnp.float32)
    for chol_ref in chol_refs:
        def per_vector(g, carry, chol_ref=chol_ref):
            vector = chol_ref[g]
            for s in range(n_slot):
                blocks = jnp.dot(vector, theta_ref[s], preferred_element_type=jnp.float32)
                crossed_ref[s] += blocks * blocks.T
                diag = jnp.sum(jnp.where(diagonal, blocks, 0.0), axis=0, keepdims=True)
                trace = jnp.sum(diag, axis=1, keepdims=True)
                square_ref[pl.ds(s, 1), :] += jnp.broadcast_to(trace * trace, (1, lanes))
            return carry

        lax.fori_loop(0, chol_ref.shape[0], per_vector, 0)
    for s in range(n_slot):
        crossed = jnp.sum(crossed_ref[s], keepdims=True)
        out_ref[pl.ds(s, 1), :] = 0.5 * (square_ref[pl.ds(s, 1), :] - jnp.broadcast_to(crossed, (1, lanes)))


def block_energy(theta, pieces):
    n_slot, _, electrons = theta.shape
    vmem = pltpu.MemorySpace.VMEM
    held = sum(p.size * p.dtype.itemsize for p in pieces) + theta.size * theta.dtype.itemsize
    out = pl.pallas_call(
        energy_kernel,
        out_shape=jax.ShapeDtypeStruct((n_slot, 128), jnp.float32),
        in_specs=[pl.BlockSpec(memory_space=vmem)] * (1 + len(pieces)),
        out_specs=pl.BlockSpec(memory_space=vmem),
        scratch_shapes=[
            pltpu.VMEM((n_slot, electrons, electrons), jnp.float32),
            pltpu.VMEM((n_slot, 128), jnp.float32),
        ],
        compiler_params=pltpu.CompilerParams(vmem_limit_bytes=int(held + (16 << 20))),
    )(theta, *pieces)
    return out[:, 0]


def swap_pairs(x, axis, size, bit):
    perm = [(i, i ^ bit) for i in range(size)]
    return lax.ppermute(x, axis, perm)


def kick_kernel(source_ref, living_ref, *refs):
    walker_refs = refs[:4]
    field_ref, new_ref, theta_ref, buffer, copy_sem = refs[4:]
    s = pl.program_id(0)
    old_dev = walker_refs[0].shape[0]
    source = source_ref[s]
    for r, walker_ref in enumerate(walker_refs):
        @pl.when(source // old_dev == r)
        def _(walker_ref=walker_ref):
            copy = pltpu.make_async_copy(walker_ref.at[source % old_dev], buffer, copy_sem)
            copy.start()
            copy.wait()

    orbitals, electrons = buffer.shape
    lanes = field_ref.shape[0]
    scale = jnp.transpose(jnp.exp(field_ref[...]))
    pick = lax.broadcasted_iota(jnp.int32, scale.shape, 1) == s
    scale = jnp.sum(jnp.where(pick, scale, 0.0), axis=1, keepdims=True)
    kicked = (scale * buffer[...].astype(jnp.float32)).astype(jnp.bfloat16)
    live = living_ref[s] > 0
    new_ref[0] = jnp.where(live, kicked, jnp.zeros_like(kicked))

    widened = kicked.astype(jnp.float32)
    intersection = widened[:electrons, :]
    rows = lax.broadcasted_iota(jnp.int32, (electrons, electrons), 0)
    cols = lax.broadcasted_iota(jnp.int32, (electrons, electrons), 1)
    eye = rows == cols
    identity = eye.astype(jnp.float32)
    diagonal = jnp.sum(jnp.where(eye, intersection, 0.0), axis=0, keepdims=True)
    inverse = jnp.where(eye, 1.0 / diagonal, 0.0)
    for sweep in range(ITERS):
        product = jnp.dot(intersection, inverse, precision=lax.Precision.HIGHEST, preferred_element_type=jnp.float32)
        inverse = jnp.dot(inverse, 2.0 * identity - product, precision=lax.Precision.HIGHEST, preferred_element_type=jnp.float32)
    theta = jnp.dot(widened, inverse, precision=lax.Precision.HIGHEST, preferred_element_type=jnp.float32)
    theta_ref[0] = theta.astype(jnp.bfloat16)


def kick(old_walkers, beside, across, diagonal_peer, parent, field, walk_id):
    old_dev, orbitals, electrons = old_walkers.shape
    slot_dev = parent.shape[0]
    living = (parent >= 0).astype(jnp.int32)
    source = jnp.maximum(parent, 0)
    relative = (source // old_dev) ^ walk_id
    index = (relative * old_dev + source % old_dev).astype(jnp.int32)
    lanes = max(8, -(-slot_dev // 8) * 8)
    padded = jnp.zeros((lanes, orbitals), jnp.float32).at[:slot_dev].set(field)
    any_space = pl.BlockSpec(memory_space=pl.ANY)
    slot_block = pl.BlockSpec((1, orbitals, electrons), lambda s, *_: (s, 0, 0))
    grid_spec = pltpu.PrefetchScalarGridSpec(
        num_scalar_prefetch=2,
        grid=(slot_dev,),
        in_specs=[any_space] * 4 + [pl.BlockSpec((lanes, orbitals), lambda s, *_: (0, 0))],
        out_specs=[slot_block, slot_block],
        scratch_shapes=[pltpu.VMEM((orbitals, electrons), old_walkers.dtype), pltpu.SemaphoreType.DMA(())],
    )
    shape = jax.ShapeDtypeStruct((slot_dev, orbitals, electrons), jnp.bfloat16)
    new_walkers, theta = pl.pallas_call(
        kick_kernel,
        out_shape=[shape, shape],
        grid_spec=grid_spec,
    )(index, living, old_walkers, beside, across, diagonal_peer, padded)
    return new_walkers, theta


def body(old_walkers, half_chol, parent, field):
    n_walk = lax.axis_size("walk")
    walk_id = lax.axis_index("walk")
    core = walk_id % 2

    across = swap_pairs(old_walkers, "walk", n_walk, 2)
    beside = swap_pairs(old_walkers, "walk", n_walk, 1)

    local_g = half_chol.shape[0]
    half_g = local_g // 2
    mine = lax.dynamic_slice_in_dim(half_chol, core * half_g, half_g, axis=0)
    n_chol = lax.axis_size("chol")
    order = list(range(0, n_chol, 2)) + list(range(n_chol - 1, 0, -2))
    forward = [(order[i], order[(i + 1) % n_chol]) for i in range(n_chol)]
    backward = [(b, a) for a, b in forward]
    n_forward = n_chol // 2
    n_backward = n_chol - 1 - n_forward
    walker_step = max(n_forward - 2, 0)
    pieces = []
    handed = []
    ahead = mine
    behind = mine
    new_walkers = theta = None
    for step in range(n_forward):
        ahead = lax.ppermute(ahead, "chol", forward)
        carried = [ahead]
        if step < n_backward:
            behind = lax.ppermute(behind, "chol", backward)
            carried.append(behind)
        if step == walker_step:
            carried += [across, beside]
        if step == n_forward - 1:
            diagonal_peer = swap_pairs(across, "walk", n_walk, 1)
            new_walkers, theta = kick(old_walkers, beside, across, diagonal_peer, parent, field, walk_id)
            carried += [new_walkers, theta]
        carried = list(lax.optimization_barrier(tuple(carried)))
        ahead = carried.pop(0)
        arrived = [ahead]
        if step < n_backward:
            behind = carried.pop(0)
            arrived.append(behind)
        if step == walker_step:
            across, beside = carried.pop(0), carried.pop(0)
        if step == n_forward - 1:
            new_walkers, theta = carried.pop(0), carried.pop(0)
        for piece in arrived:
            pieces.append(piece)
            handed.append(swap_pairs(piece, "walk", n_walk, 1))
    if theta is None:
        diagonal_peer = swap_pairs(across, "walk", n_walk, 1)
        new_walkers, theta = kick(old_walkers, beside, across, diagonal_peer, parent, field, walk_id)

    living = parent >= 0
    energy = block_energy(theta, [half_chol] + pieces + handed)
    energy = jnp.where(living, energy, 0.0)
    return (new_walkers, energy)


def solution(mesh):
    return jax.shard_map(
        body,
        mesh=mesh,
        in_specs=(
            P(("walk", "chol"), None, None),
            P("chol", None, None),
            P(("walk", "chol")),
            P(("walk", "chol"), None),
        ),
        out_specs=(P(("walk", "chol"), None, None), P(("walk", "chol"))),
        check_vma=False,
    )
```

```python
import jax
import jax.numpy as jnp
from jax import lax
from jax.sharding import PartitionSpec as P
from jax.experimental import pallas as pl
from jax.experimental.pallas import tpu as pltpu

ITERS = 3


def green_half(walkers):
    widened = walkers.astype(jnp.float32)
    electrons = walkers.shape[2]
    intersection = widened[:, :electrons, :]
    identity = jnp.eye(electrons, dtype=jnp.float32)
    diagonal = jnp.diagonal(intersection, axis1=1, axis2=2)
    inverse = identity[None, :, :] / diagonal[:, None, :]
    for sweep in range(ITERS):
        product = jnp.einsum("wij,wjk->wik", intersection, inverse, precision=lax.Precision.HIGHEST)
        inverse = jnp.einsum(
            "wij,wjk->wik",
            inverse,
            2.0 * identity[None, :, :] - product,
            precision=lax.Precision.HIGHEST,
        )
    theta = jnp.einsum("wnk,wkj->wnj", widened, inverse, precision=lax.Precision.HIGHEST)
    return theta.astype(jnp.bfloat16)


def energy_kernel(*refs):
    theta_ref = refs[0]
    chol_refs = refs[1:-3]
    out_ref, crossed_ref, square_ref = refs[-3:]
    n_slot, _, electrons = theta_ref.shape
    lanes = out_ref.shape[1]
    rows = lax.broadcasted_iota(jnp.int32, (electrons, electrons), 0)
    cols = lax.broadcasted_iota(jnp.int32, (electrons, electrons), 1)
    diagonal = rows == cols
    crossed_ref[...] = jnp.zeros(crossed_ref.shape, jnp.float32)
    square_ref[...] = jnp.zeros(square_ref.shape, jnp.float32)
    for chol_ref in chol_refs:
        def per_vector(g, carry, chol_ref=chol_ref):
            vector = chol_ref[g]
            for s in range(n_slot):
                blocks = jnp.dot(vector, theta_ref[s], preferred_element_type=jnp.float32)
                crossed_ref[s] += blocks * blocks.T
                diag = jnp.sum(jnp.where(diagonal, blocks, 0.0), axis=0, keepdims=True)
                trace = jnp.sum(diag, axis=1, keepdims=True)
                square_ref[pl.ds(s, 1), :] += jnp.broadcast_to(trace * trace, (1, lanes))
            return carry

        lax.fori_loop(0, chol_ref.shape[0], per_vector, 0)
    for s in range(n_slot):
        crossed = jnp.sum(crossed_ref[s], keepdims=True)
        out_ref[pl.ds(s, 1), :] = 0.5 * (square_ref[pl.ds(s, 1), :] - jnp.broadcast_to(crossed, (1, lanes)))


def block_energy(theta, pieces):
    n_slot, _, electrons = theta.shape
    vmem = pltpu.MemorySpace.VMEM
    held = sum(p.size * p.dtype.itemsize for p in pieces) + theta.size * theta.dtype.itemsize
    out = pl.pallas_call(
        energy_kernel,
        out_shape=jax.ShapeDtypeStruct((n_slot, 128), jnp.float32),
        in_specs=[pl.BlockSpec(memory_space=vmem)] * (1 + len(pieces)),
        out_specs=pl.BlockSpec(memory_space=vmem),
        scratch_shapes=[
            pltpu.VMEM((n_slot, electrons, electrons), jnp.float32),
            pltpu.VMEM((n_slot, 128), jnp.float32),
        ],
        compiler_params=pltpu.CompilerParams(vmem_limit_bytes=int(held + (16 << 20))),
    )(theta, *pieces)
    return out[:, 0]


def swap_pairs(x, axis, size, bit):
    perm = [(i, i ^ bit) for i in range(size)]
    return lax.ppermute(x, axis, perm)


def kick_kernel(source_ref, living_ref, *refs):
    walker_refs = refs[:4]
    field_ref, new_ref, kicked_ref, buffer, copy_sem = refs[4:]
    s = pl.program_id(0)
    old_dev = walker_refs[0].shape[0]
    source = source_ref[s]
    for r, walker_ref in enumerate(walker_refs):
        @pl.when(source // old_dev == r)
        def _(walker_ref=walker_ref):
            copy = pltpu.make_async_copy(walker_ref.at[source % old_dev], buffer, copy_sem)
            copy.start()
            copy.wait()

    orbitals, electrons = buffer.shape
    lanes = field_ref.shape[0]
    scale = jnp.transpose(jnp.exp(field_ref[...]))
    pick = lax.broadcasted_iota(jnp.int32, scale.shape, 1) == s
    scale = jnp.sum(jnp.where(pick, scale, 0.0), axis=1, keepdims=True)
    kicked = (scale * buffer[...].astype(jnp.float32)).astype(jnp.bfloat16)
    live = living_ref[s] > 0
    new_ref[0] = jnp.where(live, kicked, jnp.zeros_like(kicked))

    kicked_ref[0] = kicked


def kick(old_walkers, beside, across, diagonal_peer, parent, field, walk_id):
    old_dev, orbitals, electrons = old_walkers.shape
    slot_dev = parent.shape[0]
    living = (parent >= 0).astype(jnp.int32)
    source = jnp.maximum(parent, 0)
    relative = (source // old_dev) ^ walk_id
    index = (relative * old_dev + source % old_dev).astype(jnp.int32)
    lanes = max(8, -(-slot_dev // 8) * 8)
    padded = jnp.zeros((lanes, orbitals), jnp.float32).at[:slot_dev].set(field)
    any_space = pl.BlockSpec(memory_space=pl.ANY)
    slot_block = pl.BlockSpec((1, orbitals, electrons), lambda s, *_: (s, 0, 0))
    grid_spec = pltpu.PrefetchScalarGridSpec(
        num_scalar_prefetch=2,
        grid=(slot_dev,),
        in_specs=[any_space] * 4 + [pl.BlockSpec((lanes, orbitals), lambda s, *_: (0, 0))],
        out_specs=[slot_block, slot_block],
        scratch_shapes=[pltpu.VMEM((orbitals, electrons), old_walkers.dtype), pltpu.SemaphoreType.DMA(())],
    )
    shape = jax.ShapeDtypeStruct((slot_dev, orbitals, electrons), jnp.bfloat16)
    new_walkers, kicked = pl.pallas_call(
        kick_kernel,
        out_shape=[shape, shape],
        grid_spec=grid_spec,
    )(index, living, old_walkers, beside, across, diagonal_peer, padded)
    return new_walkers, green_half(kicked)


def body(old_walkers, half_chol, parent, field):
    n_walk = lax.axis_size("walk")
    walk_id = lax.axis_index("walk")
    core = walk_id % 2

    across = swap_pairs(old_walkers, "walk", n_walk, 2)
    beside = swap_pairs(old_walkers, "walk", n_walk, 1)

    local_g = half_chol.shape[0]
    half_g = local_g // 2
    mine = lax.dynamic_slice_in_dim(half_chol, core * half_g, half_g, axis=0)
    n_chol = lax.axis_size("chol")
    order = list(range(0, n_chol, 2)) + list(range(n_chol - 1, 0, -2))
    forward = [(order[i], order[(i + 1) % n_chol]) for i in range(n_chol)]
    backward = [(b, a) for a, b in forward]
    n_forward = n_chol // 2
    n_backward = n_chol - 1 - n_forward
    walker_step = max(n_forward - 2, 0)
    pieces = []
    handed = []
    ahead = mine
    behind = mine
    new_walkers = theta = None
    for step in range(n_forward):
        ahead = lax.ppermute(ahead, "chol", forward)
        carried = [ahead]
        if step < n_backward:
            behind = lax.ppermute(behind, "chol", backward)
            carried.append(behind)
        if step == walker_step:
            carried += [across, beside]
        if step == n_forward - 1:
            diagonal_peer = swap_pairs(across, "walk", n_walk, 1)
            new_walkers, theta = kick(old_walkers, beside, across, diagonal_peer, parent, field, walk_id)
            carried += [new_walkers, theta]
        carried = list(lax.optimization_barrier(tuple(carried)))
        ahead = carried.pop(0)
        arrived = [ahead]
        if step < n_backward:
            behind = carried.pop(0)
            arrived.append(behind)
        if step == walker_step:
            across, beside = carried.pop(0), carried.pop(0)
        if step == n_forward - 1:
            new_walkers, theta = carried.pop(0), carried.pop(0)
        for piece in arrived:
            pieces.append(piece)
            handed.append(swap_pairs(piece, "walk", n_walk, 1))
    if theta is None:
        diagonal_peer = swap_pairs(across, "walk", n_walk, 1)
        new_walkers, theta = kick(old_walkers, beside, across, diagonal_peer, parent, field, walk_id)

    living = parent >= 0
    energy = block_energy(theta, [half_chol] + pieces + handed)
    energy = jnp.where(living, energy, 0.0)
    return (new_walkers, energy)


def solution(mesh):
    return jax.shard_map(
        body,
        mesh=mesh,
        in_specs=(
            P(("walk", "chol"), None, None),
            P("chol", None, None),
            P(("walk", "chol")),
            P(("walk", "chol"), None),
        ),
        out_specs=(P(("walk", "chol"), None, None), P(("walk", "chol"))),
        check_vma=False,
    )
```

```python
import jax
import jax.numpy as jnp
from jax import lax
from jax.sharding import PartitionSpec as P
from jax.experimental import pallas as pl
from jax.experimental.pallas import tpu as pltpu

ITERS = 3


def green_half(walkers):
    widened = walkers.astype(jnp.float32)
    electrons = walkers.shape[2]
    intersection = widened[:, :electrons, :]
    identity = jnp.eye(electrons, dtype=jnp.float32)
    diagonal = jnp.diagonal(intersection, axis1=1, axis2=2)
    inverse = identity[None, :, :] / diagonal[:, None, :]
    for sweep in range(ITERS):
        product = jnp.einsum("wij,wjk->wik", intersection, inverse, precision=lax.Precision.HIGHEST)
        inverse = jnp.einsum(
            "wij,wjk->wik",
            inverse,
            2.0 * identity[None, :, :] - product,
            precision=lax.Precision.HIGHEST,
        )
    theta = jnp.einsum("wnk,wkj->wnj", widened, inverse, precision=lax.Precision.HIGHEST)
    return theta.astype(jnp.bfloat16)


def energy_kernel(*refs):
    theta_ref = refs[0]
    chol_refs = refs[1:-3]
    out_ref, crossed_ref, square_ref = refs[-3:]
    n_slot, _, electrons = theta_ref.shape
    lanes = out_ref.shape[1]
    rows = lax.broadcasted_iota(jnp.int32, (electrons, electrons), 0)
    cols = lax.broadcasted_iota(jnp.int32, (electrons, electrons), 1)
    diagonal = rows == cols
    crossed_ref[...] = jnp.zeros(crossed_ref.shape, jnp.float32)
    square_ref[...] = jnp.zeros(square_ref.shape, jnp.float32)
    for chol_ref in chol_refs:
        def per_vector(g, carry, chol_ref=chol_ref):
            vector = chol_ref[g]
            for s in range(n_slot):
                blocks = jnp.dot(vector, theta_ref[s], preferred_element_type=jnp.float32)
                crossed_ref[s] += blocks * blocks.T
                diag = jnp.sum(jnp.where(diagonal, blocks, 0.0), axis=0, keepdims=True)
                trace = jnp.sum(diag, axis=1, keepdims=True)
                square_ref[pl.ds(s, 1), :] += jnp.broadcast_to(trace * trace, (1, lanes))
            return carry

        lax.fori_loop(0, chol_ref.shape[0], per_vector, 0)
    for s in range(n_slot):
        crossed = jnp.sum(crossed_ref[s], keepdims=True)
        out_ref[pl.ds(s, 1), :] = 0.5 * (square_ref[pl.ds(s, 1), :] - jnp.broadcast_to(crossed, (1, lanes)))


def block_energy(theta, pieces):
    n_slot, _, electrons = theta.shape
    vmem = pltpu.MemorySpace.VMEM
    held = sum(p.size * p.dtype.itemsize for p in pieces) + theta.size * theta.dtype.itemsize
    out = pl.pallas_call(
        energy_kernel,
        out_shape=jax.ShapeDtypeStruct((n_slot, 128), jnp.float32),
        in_specs=[pl.BlockSpec(memory_space=vmem)] * (1 + len(pieces)),
        out_specs=pl.BlockSpec(memory_space=vmem),
        scratch_shapes=[
            pltpu.VMEM((n_slot, electrons, electrons), jnp.float32),
            pltpu.VMEM((n_slot, 128), jnp.float32),
        ],
        compiler_params=pltpu.CompilerParams(vmem_limit_bytes=int(held + (16 << 20))),
    )(theta, *pieces)
    return out[:, 0]


def swap_pairs(x, axis, size, bit):
    perm = [(i, i ^ bit) for i in range(size)]
    return lax.ppermute(x, axis, perm)


def kick_kernel(source_ref, living_ref, *refs):
    walker_refs = refs[:4]
    scale_ref, new_ref, kicked_ref, buffer, copy_sem = refs[4:]
    s = pl.program_id(0)
    old_dev = walker_refs[0].shape[0]
    source = source_ref[s]
    for r, walker_ref in enumerate(walker_refs):
        @pl.when(source // old_dev == r)
        def _(walker_ref=walker_ref):
            copy = pltpu.make_async_copy(walker_ref.at[source % old_dev], buffer, copy_sem)
            copy.start()
            copy.wait()

    kicked = (scale_ref[0] * buffer[...].astype(jnp.float32)).astype(jnp.bfloat16)
    live = living_ref[s] > 0
    new_ref[0] = jnp.where(live, kicked, jnp.zeros_like(kicked))

    kicked_ref[0] = kicked


def kick(old_walkers, beside, across, diagonal_peer, parent, field, walk_id):
    old_dev, orbitals, electrons = old_walkers.shape
    slot_dev = parent.shape[0]
    living = (parent >= 0).astype(jnp.int32)
    source = jnp.maximum(parent, 0)
    relative = (source // old_dev) ^ walk_id
    index = (relative * old_dev + source % old_dev).astype(jnp.int32)
    scale = jnp.broadcast_to(jnp.exp(field)[:, :, None], (slot_dev, orbitals, electrons))
    any_space = pl.BlockSpec(memory_space=pl.ANY)
    slot_block = pl.BlockSpec((1, orbitals, electrons), lambda s, *_: (s, 0, 0))
    grid_spec = pltpu.PrefetchScalarGridSpec(
        num_scalar_prefetch=2,
        grid=(slot_dev,),
        in_specs=[any_space] * 4 + [pl.BlockSpec((1, orbitals, electrons), lambda s, *_: (s, 0, 0))],
        out_specs=[slot_block, slot_block],
        scratch_shapes=[pltpu.VMEM((orbitals, electrons), old_walkers.dtype), pltpu.SemaphoreType.DMA(())],
    )
    shape = jax.ShapeDtypeStruct((slot_dev, orbitals, electrons), jnp.bfloat16)
    new_walkers, kicked = pl.pallas_call(
        kick_kernel,
        out_shape=[shape, shape],
        grid_spec=grid_spec,
    )(index, living, old_walkers, beside, across, diagonal_peer, scale)
    return new_walkers, green_half(kicked)


def body(old_walkers, half_chol, parent, field):
    n_walk = lax.axis_size("walk")
    walk_id = lax.axis_index("walk")
    core = walk_id % 2

    across = swap_pairs(old_walkers, "walk", n_walk, 2)
    beside = swap_pairs(old_walkers, "walk", n_walk, 1)

    local_g = half_chol.shape[0]
    half_g = local_g // 2
    mine = lax.dynamic_slice_in_dim(half_chol, core * half_g, half_g, axis=0)
    n_chol = lax.axis_size("chol")
    order = list(range(0, n_chol, 2)) + list(range(n_chol - 1, 0, -2))
    forward = [(order[i], order[(i + 1) % n_chol]) for i in range(n_chol)]
    backward = [(b, a) for a, b in forward]
    n_forward = n_chol // 2
    n_backward = n_chol - 1 - n_forward
    walker_step = max(n_forward - 2, 0)
    pieces = []
    handed = []
    ahead = mine
    behind = mine
    new_walkers = theta = None
    for step in range(n_forward):
        ahead = lax.ppermute(ahead, "chol", forward)
        carried = [ahead]
        if step < n_backward:
            behind = lax.ppermute(behind, "chol", backward)
            carried.append(behind)
        if step == walker_step:
            carried += [across, beside]
        if step == n_forward - 1:
            diagonal_peer = swap_pairs(across, "walk", n_walk, 1)
            new_walkers, theta = kick(old_walkers, beside, across, diagonal_peer, parent, field, walk_id)
            carried += [new_walkers, theta]
        carried = list(lax.optimization_barrier(tuple(carried)))
        ahead = carried.pop(0)
        arrived = [ahead]
        if step < n_backward:
            behind = carried.pop(0)
            arrived.append(behind)
        if step == walker_step:
            across, beside = carried.pop(0), carried.pop(0)
        if step == n_forward - 1:
            new_walkers, theta = carried.pop(0), carried.pop(0)
        for piece in arrived:
            pieces.append(piece)
            handed.append(swap_pairs(piece, "walk", n_walk, 1))
    if theta is None:
        diagonal_peer = swap_pairs(across, "walk", n_walk, 1)
        new_walkers, theta = kick(old_walkers, beside, across, diagonal_peer, parent, field, walk_id)

    living = parent >= 0
    energy = block_energy(theta, [half_chol] + pieces + handed)
    energy = jnp.where(living, energy, 0.0)
    return (new_walkers, energy)


def solution(mesh):
    return jax.shard_map(
        body,
        mesh=mesh,
        in_specs=(
            P(("walk", "chol"), None, None),
            P("chol", None, None),
            P(("walk", "chol")),
            P(("walk", "chol"), None),
        ),
        out_specs=(P(("walk", "chol"), None, None), P(("walk", "chol"))),
        check_vma=False,
    )
```

```python
import jax
import jax.numpy as jnp
from jax import lax
from jax.sharding import PartitionSpec as P
from jax.experimental import pallas as pl
from jax.experimental.pallas import tpu as pltpu

ITERS = 3


def green_half(walkers):
    widened = walkers.astype(jnp.float32)
    electrons = walkers.shape[2]
    intersection = widened[:, :electrons, :]
    identity = jnp.eye(electrons, dtype=jnp.float32)
    diagonal = jnp.diagonal(intersection, axis1=1, axis2=2)
    inverse = identity[None, :, :] / diagonal[:, None, :]
    for sweep in range(ITERS):
        product = jnp.einsum("wij,wjk->wik", intersection, inverse, precision=lax.Precision.HIGHEST)
        inverse = jnp.einsum(
            "wij,wjk->wik",
            inverse,
            2.0 * identity[None, :, :] - product,
            precision=lax.Precision.HIGHEST,
        )
    theta = jnp.einsum("wnk,wkj->wnj", widened, inverse, precision=lax.Precision.HIGHEST)
    return theta.astype(jnp.bfloat16)


def energy_kernel(*refs):
    theta_ref = refs[0]
    chol_refs = refs[1:-3]
    out_ref, crossed_ref, square_ref = refs[-3:]
    n_slot, _, electrons = theta_ref.shape
    lanes = out_ref.shape[1]
    rows = lax.broadcasted_iota(jnp.int32, (electrons, electrons), 0)
    cols = lax.broadcasted_iota(jnp.int32, (electrons, electrons), 1)
    diagonal = rows == cols
    crossed_ref[...] = jnp.zeros(crossed_ref.shape, jnp.float32)
    square_ref[...] = jnp.zeros(square_ref.shape, jnp.float32)
    for chol_ref in chol_refs:
        def per_vector(g, carry, chol_ref=chol_ref):
            vector = chol_ref[g]
            for s in range(n_slot):
                blocks = jnp.dot(vector, theta_ref[s], preferred_element_type=jnp.float32)
                crossed_ref[s] += blocks * blocks.T
                diag = jnp.sum(jnp.where(diagonal, blocks, 0.0), axis=0, keepdims=True)
                trace = jnp.sum(diag, axis=1, keepdims=True)
                square_ref[pl.ds(s, 1), :] += jnp.broadcast_to(trace * trace, (1, lanes))
            return carry

        lax.fori_loop(0, chol_ref.shape[0], per_vector, 0)
    for s in range(n_slot):
        crossed = jnp.sum(crossed_ref[s], keepdims=True)
        out_ref[pl.ds(s, 1), :] = 0.5 * (square_ref[pl.ds(s, 1), :] - jnp.broadcast_to(crossed, (1, lanes)))


def block_energy(theta, pieces):
    n_slot, _, electrons = theta.shape
    vmem = pltpu.MemorySpace.VMEM
    held = sum(p.size * p.dtype.itemsize for p in pieces) + theta.size * theta.dtype.itemsize
    out = pl.pallas_call(
        energy_kernel,
        out_shape=jax.ShapeDtypeStruct((n_slot, 128), jnp.float32),
        in_specs=[pl.BlockSpec(memory_space=vmem)] * (1 + len(pieces)),
        out_specs=pl.BlockSpec(memory_space=vmem),
        scratch_shapes=[
            pltpu.VMEM((n_slot, electrons, electrons), jnp.float32),
            pltpu.VMEM((n_slot, 128), jnp.float32),
        ],
        compiler_params=pltpu.CompilerParams(vmem_limit_bytes=int(held + (16 << 20))),
    )(theta, *pieces)
    return out[:, 0]


def swap_pairs(x, axis, size, bit):
    perm = [(i, i ^ bit) for i in range(size)]
    return lax.ppermute(x, axis, perm)


def kick_kernel(source_ref, living_ref, *refs):
    walker_refs = refs[:4]
    field_ref, new_hbm, theta_hbm, walkers, kicked_buf, new_buf, theta_buf, in_sem, out_sem = refs[4:]
    old_dev = walker_refs[0].shape[0]
    n_slot, orbitals, electrons = walkers.shape

    for s in range(n_slot):
        source = source_ref[s]
        for r, walker_ref in enumerate(walker_refs):
            group = source // old_dev
            chosen = group >= r if r == len(walker_refs) - 1 else group == r

            @pl.when(chosen)
            def _(walker_ref=walker_ref, source=source, s=s):
                pltpu.make_async_copy(walker_ref.at[source % old_dev], walkers.at[s], in_sem.at[s]).start()

    scale_all = jnp.transpose(jnp.exp(field_ref[...]))
    rows = lax.broadcasted_iota(jnp.int32, (electrons, electrons), 0)
    cols = lax.broadcasted_iota(jnp.int32, (electrons, electrons), 1)
    eye = rows == cols
    identity = eye.astype(jnp.float32)
    out_copies = []
    intersections = []
    inverses = []
    for s in range(n_slot):
        pltpu.make_async_copy(walker_refs[0].at[0], walkers.at[s], in_sem.at[s]).wait()
        kicked = (scale_all[:, s:s + 1] * walkers[s].astype(jnp.float32)).astype(jnp.bfloat16)
        kicked_buf[s] = kicked
        new_buf[s] = jnp.where(living_ref[s] > 0, kicked, jnp.zeros_like(kicked))
        copy = pltpu.make_async_copy(new_buf.at[s], new_hbm.at[s], out_sem.at[0, s])
        copy.start()
        out_copies.append(copy)
        intersection = kicked[:electrons, :].astype(jnp.float32)
        diagonal = jnp.sum(jnp.where(eye, intersection, 0.0), axis=0, keepdims=True)
        intersections.append(intersection)
        inverses.append(jnp.where(eye, 1.0 / diagonal, 0.0))

    for sweep in range(ITERS):
        products = [
            jnp.dot(x, inv, precision=lax.Precision.HIGHEST, preferred_element_type=jnp.float32)
            for x, inv in zip(intersections, inverses)
        ]
        inverses = [
            jnp.dot(inv, 2.0 * identity - p, precision=lax.Precision.HIGHEST, preferred_element_type=jnp.float32)
            for inv, p in zip(inverses, products)
        ]

    for s in range(n_slot):
        widened = kicked_buf[s].astype(jnp.float32)
        theta = jnp.dot(widened, inverses[s], precision=lax.Precision.HIGHEST, preferred_element_type=jnp.float32)
        theta_buf[s] = theta.astype(jnp.bfloat16)
        copy = pltpu.make_async_copy(theta_buf.at[s], theta_hbm.at[s], out_sem.at[1, s])
        copy.start()
        out_copies.append(copy)
    for copy in out_copies:
        copy.wait()


def kick(old_walkers, beside, across, diagonal_peer, parent, field, walk_id):
    old_dev, orbitals, electrons = old_walkers.shape
    slot_dev = parent.shape[0]
    living = (parent >= 0).astype(jnp.int32)
    source = jnp.maximum(parent, 0)
    relative = (source // old_dev) ^ walk_id
    index = (relative * old_dev + source % old_dev).astype(jnp.int32)
    lanes = max(8, -(-slot_dev // 8) * 8)
    padded = jnp.zeros((lanes, orbitals), jnp.float32).at[:slot_dev].set(field)
    any_space = pl.BlockSpec(memory_space=pl.ANY)
    slots = (slot_dev, orbitals, electrons)
    grid_spec = pltpu.PrefetchScalarGridSpec(
        num_scalar_prefetch=2,
        grid=(1,),
        in_specs=[any_space] * 4 + [pl.BlockSpec((lanes, orbitals), lambda i, *_: (0, 0))],
        out_specs=[any_space, any_space],
        scratch_shapes=[
            pltpu.VMEM(slots, jnp.bfloat16),
            pltpu.VMEM(slots, jnp.bfloat16),
            pltpu.VMEM(slots, jnp.bfloat16),
            pltpu.VMEM(slots, jnp.bfloat16),
            pltpu.SemaphoreType.DMA((slot_dev,)),
            pltpu.SemaphoreType.DMA((2, slot_dev)),
        ],
    )
    shape = jax.ShapeDtypeStruct(slots, jnp.bfloat16)
    new_walkers, theta = pl.pallas_call(
        kick_kernel,
        out_shape=[shape, shape],
        grid_spec=grid_spec,
    )(index, living, old_walkers, beside, across, diagonal_peer, padded)
    return new_walkers, theta


def body(old_walkers, half_chol, parent, field):
    n_walk = lax.axis_size("walk")
    walk_id = lax.axis_index("walk")
    core = walk_id % 2

    across = swap_pairs(old_walkers, "walk", n_walk, 2)
    beside = swap_pairs(old_walkers, "walk", n_walk, 1)

    local_g = half_chol.shape[0]
    half_g = local_g // 2
    mine = lax.dynamic_slice_in_dim(half_chol, core * half_g, half_g, axis=0)
    n_chol = lax.axis_size("chol")
    order = list(range(0, n_chol, 2)) + list(range(n_chol - 1, 0, -2))
    forward = [(order[i], order[(i + 1) % n_chol]) for i in range(n_chol)]
    backward = [(b, a) for a, b in forward]
    n_forward = n_chol // 2
    n_backward = n_chol - 1 - n_forward
    walker_step = max(n_forward - 2, 0)
    pieces = []
    handed = []
    ahead = mine
    behind = mine
    new_walkers = theta = None
    for step in range(n_forward):
        ahead = lax.ppermute(ahead, "chol", forward)
        carried = [ahead]
        if step < n_backward:
            behind = lax.ppermute(behind, "chol", backward)
            carried.append(behind)
        if step == walker_step:
            carried += [across, beside]
        if step == n_forward - 1:
            diagonal_peer = swap_pairs(across, "walk", n_walk, 1)
            new_walkers, theta = kick(old_walkers, beside, across, diagonal_peer, parent, field, walk_id)
            carried += [new_walkers, theta]
        carried = list(lax.optimization_barrier(tuple(carried)))
        ahead = carried.pop(0)
        arrived = [ahead]
        if step < n_backward:
            behind = carried.pop(0)
            arrived.append(behind)
        if step == walker_step:
            across, beside = carried.pop(0), carried.pop(0)
        if step == n_forward - 1:
            new_walkers, theta = carried.pop(0), carried.pop(0)
        for piece in arrived:
            pieces.append(piece)
            handed.append(swap_pairs(piece, "walk", n_walk, 1))
    if theta is None:
        diagonal_peer = swap_pairs(across, "walk", n_walk, 1)
        new_walkers, theta = kick(old_walkers, beside, across, diagonal_peer, parent, field, walk_id)

    living = parent >= 0
    energy = block_energy(theta, [half_chol] + pieces + handed)
    energy = jnp.where(living, energy, 0.0)
    return (new_walkers, energy)


def solution(mesh):
    return jax.shard_map(
        body,
        mesh=mesh,
        in_specs=(
            P(("walk", "chol"), None, None),
            P("chol", None, None),
            P(("walk", "chol")),
            P(("walk", "chol"), None),
        ),
        out_specs=(P(("walk", "chol"), None, None), P(("walk", "chol"))),
        check_vma=False,
    )
```

```python
import jax
import jax.numpy as jnp
from jax import lax
from jax.sharding import PartitionSpec as P
from jax.experimental import pallas as pl
from jax.experimental.pallas import tpu as pltpu

ITERS = 3


def green_half(walkers):
    widened = walkers.astype(jnp.float32)
    electrons = walkers.shape[2]
    intersection = widened[:, :electrons, :]
    identity = jnp.eye(electrons, dtype=jnp.float32)
    diagonal = jnp.diagonal(intersection, axis1=1, axis2=2)
    inverse = identity[None, :, :] / diagonal[:, None, :]
    for sweep in range(ITERS):
        product = jnp.einsum("wij,wjk->wik", intersection, inverse, precision=lax.Precision.HIGHEST)
        inverse = jnp.einsum(
            "wij,wjk->wik",
            inverse,
            2.0 * identity[None, :, :] - product,
            precision=lax.Precision.HIGHEST,
        )
    theta = jnp.einsum("wnk,wkj->wnj", widened, inverse, precision=lax.Precision.HIGHEST)
    return theta.astype(jnp.bfloat16)


def energy_kernel(*refs):
    theta_ref = refs[0]
    chol_refs = refs[1:-3]
    out_ref, crossed_ref, square_ref = refs[-3:]
    n_slot, _, electrons = theta_ref.shape
    lanes = out_ref.shape[1]
    rows = lax.broadcasted_iota(jnp.int32, (electrons, electrons), 0)
    cols = lax.broadcasted_iota(jnp.int32, (electrons, electrons), 1)
    diagonal = rows == cols
    crossed_ref[...] = jnp.zeros(crossed_ref.shape, jnp.float32)
    square_ref[...] = jnp.zeros(square_ref.shape, jnp.float32)
    for chol_ref in chol_refs:
        def per_vector(g, carry, chol_ref=chol_ref):
            vector = chol_ref[g]
            for s in range(n_slot):
                blocks = jnp.dot(vector, theta_ref[s], preferred_element_type=jnp.float32)
                crossed_ref[s] += blocks * blocks.T
                diag = jnp.sum(jnp.where(diagonal, blocks, 0.0), axis=0, keepdims=True)
                trace = jnp.sum(diag, axis=1, keepdims=True)
                square_ref[pl.ds(s, 1), :] += jnp.broadcast_to(trace * trace, (1, lanes))
            return carry

        lax.fori_loop(0, chol_ref.shape[0], per_vector, 0)
    for s in range(n_slot):
        crossed = jnp.sum(crossed_ref[s], keepdims=True)
        out_ref[pl.ds(s, 1), :] = 0.5 * (square_ref[pl.ds(s, 1), :] - jnp.broadcast_to(crossed, (1, lanes)))


def block_energy(theta, pieces):
    n_slot, _, electrons = theta.shape
    vmem = pltpu.MemorySpace.VMEM
    held = sum(p.size * p.dtype.itemsize for p in pieces) + theta.size * theta.dtype.itemsize
    out = pl.pallas_call(
        energy_kernel,
        out_shape=jax.ShapeDtypeStruct((n_slot, 128), jnp.float32),
        in_specs=[pl.BlockSpec(memory_space=vmem)] * (1 + len(pieces)),
        out_specs=pl.BlockSpec(memory_space=vmem),
        scratch_shapes=[
            pltpu.VMEM((n_slot, electrons, electrons), jnp.float32),
            pltpu.VMEM((n_slot, 128), jnp.float32),
        ],
        compiler_params=pltpu.CompilerParams(vmem_limit_bytes=int(held + (16 << 20))),
    )(theta, *pieces)
    return out[:, 0]


def swap_pairs(x, axis, size, bit):
    perm = [(i, i ^ bit) for i in range(size)]
    return lax.ppermute(x, axis, perm)


def kick_kernel(source_ref, living_ref, *refs):
    walker_refs = refs[:4]
    field_ref, new_hbm, theta_hbm, walkers, kicked_buf, new_buf, theta_buf, in_sem, out_sem = refs[4:]
    old_dev = walker_refs[0].shape[0]
    n_slot, orbitals, electrons = walkers.shape

    for s in range(n_slot):
        source = source_ref[s]
        for r, walker_ref in enumerate(walker_refs):
            group = source // old_dev
            chosen = group >= r if r == len(walker_refs) - 1 else group == r

            @pl.when(chosen)
            def _(walker_ref=walker_ref, source=source, s=s):
                pltpu.make_async_copy(walker_ref.at[source % old_dev], walkers.at[s], in_sem.at[s]).start()

    scale_all = jnp.transpose(jnp.exp(field_ref[...]))
    rows = lax.broadcasted_iota(jnp.int32, (electrons, electrons), 0)
    cols = lax.broadcasted_iota(jnp.int32, (electrons, electrons), 1)
    eye = rows == cols
    identity = eye.astype(jnp.float32)
    out_copies = []
    intersections = []
    inverses = []
    for s in range(n_slot):
        pltpu.make_async_copy(walker_refs[0].at[0], walkers.at[s], in_sem.at[s]).wait()
        kicked = (scale_all[:, s:s + 1] * walkers[s].astype(jnp.float32)).astype(jnp.bfloat16)
        kicked_buf[s] = kicked
        new_buf[s] = jnp.where(living_ref[s] > 0, kicked, jnp.zeros_like(kicked))
        copy = pltpu.make_async_copy(new_buf.at[s], new_hbm.at[s], out_sem.at[0, s])
        copy.start()
        out_copies.append(copy)
        intersection = kicked[:electrons, :].astype(jnp.float32)
        diagonal = jnp.sum(jnp.where(eye, intersection, 0.0), axis=0, keepdims=True)
        intersections.append(intersection)
        inverses.append(jnp.where(eye, 1.0 / diagonal, 0.0))

    for sweep in range(ITERS):
        products = [
            jnp.dot(x, inv, precision=lax.Precision.HIGHEST, preferred_element_type=jnp.float32)
            for x, inv in zip(intersections, inverses)
        ]
        inverses = [
            jnp.dot(inv, 2.0 * identity - p, precision=lax.Precision.HIGHEST, preferred_element_type=jnp.float32)
            for inv, p in zip(inverses, products)
        ]

    for s in range(n_slot):
        widened = kicked_buf[s].astype(jnp.float32)
        theta = jnp.dot(widened, inverses[s], precision=lax.Precision.HIGHEST, preferred_element_type=jnp.float32)
        theta_buf[s] = theta.astype(jnp.bfloat16)
        copy = pltpu.make_async_copy(theta_buf.at[s], theta_hbm.at[s], out_sem.at[1, s])
        copy.start()
        out_copies.append(copy)
    for copy in out_copies:
        copy.wait()


def kick_operands(old_dev, parent, field, walk_id):
    slot_dev, orbitals = field.shape
    living = (parent >= 0).astype(jnp.int32)
    source = jnp.maximum(parent, 0)
    relative = (source // old_dev) ^ walk_id
    index = (relative * old_dev + source % old_dev).astype(jnp.int32)
    lanes = max(8, -(-slot_dev // 8) * 8)
    padded = jnp.zeros((lanes, orbitals), jnp.float32).at[:slot_dev].set(field)
    return index, living, padded


def kick(old_walkers, beside, across, diagonal_peer, index, living, padded):
    old_dev, orbitals, electrons = old_walkers.shape
    slot_dev = index.shape[0]
    lanes = padded.shape[0]
    any_space = pl.BlockSpec(memory_space=pl.ANY)
    slots = (slot_dev, orbitals, electrons)
    grid_spec = pltpu.PrefetchScalarGridSpec(
        num_scalar_prefetch=2,
        grid=(1,),
        in_specs=[any_space] * 4 + [pl.BlockSpec((lanes, orbitals), lambda i, *_: (0, 0))],
        out_specs=[any_space, any_space],
        scratch_shapes=[
            pltpu.VMEM(slots, jnp.bfloat16),
            pltpu.VMEM(slots, jnp.bfloat16),
            pltpu.VMEM(slots, jnp.bfloat16),
            pltpu.VMEM(slots, jnp.bfloat16),
            pltpu.SemaphoreType.DMA((slot_dev,)),
            pltpu.SemaphoreType.DMA((2, slot_dev)),
        ],
    )
    shape = jax.ShapeDtypeStruct(slots, jnp.bfloat16)
    new_walkers, theta = pl.pallas_call(
        kick_kernel,
        out_shape=[shape, shape],
        grid_spec=grid_spec,
    )(index, living, old_walkers, beside, across, diagonal_peer, padded)
    return new_walkers, theta


def body(old_walkers, half_chol, parent, field):
    n_walk = lax.axis_size("walk")
    walk_id = lax.axis_index("walk")
    core = walk_id % 2

    across = swap_pairs(old_walkers, "walk", n_walk, 2)
    beside = swap_pairs(old_walkers, "walk", n_walk, 1)

    local_g = half_chol.shape[0]
    half_g = local_g // 2
    mine = lax.dynamic_slice_in_dim(half_chol, core * half_g, half_g, axis=0)
    n_chol = lax.axis_size("chol")
    order = list(range(0, n_chol, 2)) + list(range(n_chol - 1, 0, -2))
    forward = [(order[i], order[(i + 1) % n_chol]) for i in range(n_chol)]
    backward = [(b, a) for a, b in forward]
    n_forward = n_chol // 2
    n_backward = n_chol - 1 - n_forward
    walker_step = max(n_forward - 2, 0)
    pieces = []
    handed = []
    ahead = mine
    behind = mine
    new_walkers = theta = None
    operands = kick_operands(old_walkers.shape[0], parent, field, walk_id)
    for step in range(n_forward):
        ahead = lax.ppermute(ahead, "chol", forward)
        carried = [ahead]
        if step < n_backward:
            behind = lax.ppermute(behind, "chol", backward)
            carried.append(behind)
        if step == walker_step:
            carried += [across, beside]
        if step == 0:
            carried += list(operands)
        if step == n_forward - 1:
            diagonal_peer = swap_pairs(across, "walk", n_walk, 1)
            new_walkers, theta = kick(old_walkers, beside, across, diagonal_peer, *operands)
            carried += [new_walkers, theta]
        carried = list(lax.optimization_barrier(tuple(carried)))
        ahead = carried.pop(0)
        arrived = [ahead]
        if step < n_backward:
            behind = carried.pop(0)
            arrived.append(behind)
        if step == walker_step:
            across, beside = carried.pop(0), carried.pop(0)
        if step == 0:
            operands = [carried.pop(0) for item in operands]
        if step == n_forward - 1:
            new_walkers, theta = carried.pop(0), carried.pop(0)
        for piece in arrived:
            pieces.append(piece)
            handed.append(swap_pairs(piece, "walk", n_walk, 1))
    if theta is None:
        diagonal_peer = swap_pairs(across, "walk", n_walk, 1)
        new_walkers, theta = kick(old_walkers, beside, across, diagonal_peer, *operands)

    living = parent >= 0
    energy = block_energy(theta, [half_chol] + pieces + handed)
    energy = jnp.where(living, energy, 0.0)
    return (new_walkers, energy)


def solution(mesh):
    return jax.shard_map(
        body,
        mesh=mesh,
        in_specs=(
            P(("walk", "chol"), None, None),
            P("chol", None, None),
            P(("walk", "chol")),
            P(("walk", "chol"), None),
        ),
        out_specs=(P(("walk", "chol"), None, None), P(("walk", "chol"))),
        check_vma=False,
    )
```

```python
import jax
import jax.numpy as jnp
from jax import lax
from jax.sharding import PartitionSpec as P
from jax.experimental import pallas as pl
from jax.experimental.pallas import tpu as pltpu

ITERS = 3


def green_half(walkers):
    widened = walkers.astype(jnp.float32)
    electrons = walkers.shape[2]
    intersection = widened[:, :electrons, :]
    identity = jnp.eye(electrons, dtype=jnp.float32)
    diagonal = jnp.diagonal(intersection, axis1=1, axis2=2)
    inverse = identity[None, :, :] / diagonal[:, None, :]
    for sweep in range(ITERS):
        product = jnp.einsum("wij,wjk->wik", intersection, inverse, precision=lax.Precision.HIGHEST)
        inverse = jnp.einsum(
            "wij,wjk->wik",
            inverse,
            2.0 * identity[None, :, :] - product,
            precision=lax.Precision.HIGHEST,
        )
    theta = jnp.einsum("wnk,wkj->wnj", widened, inverse, precision=lax.Precision.HIGHEST)
    return theta.astype(jnp.bfloat16)


def energy_kernel(theta_ref, *refs):
    chol_refs = refs[:-1]
    out_ref = refs[-1]
    s = pl.program_id(0)
    electrons = theta_ref.shape[2]
    lanes = out_ref.shape[1]
    rows = lax.broadcasted_iota(jnp.int32, (electrons, electrons), 0)
    cols = lax.broadcasted_iota(jnp.int32, (electrons, electrons), 1)
    diagonal = rows == cols
    carry = (jnp.zeros((electrons, electrons), jnp.float32), jnp.zeros((1, 1), jnp.float32))
    for chol_ref in chol_refs:
        def per_vector(g, carry, chol_ref=chol_ref):
            crossed, square = carry
            blocks = jnp.dot(chol_ref[g], theta_ref[0], preferred_element_type=jnp.float32)
            diag = jnp.sum(jnp.where(diagonal, blocks, 0.0), axis=0, keepdims=True)
            trace = jnp.sum(diag, axis=1, keepdims=True)
            return crossed + blocks * blocks.T, square + trace * trace

        carry = lax.fori_loop(0, chol_ref.shape[0], per_vector, carry)
    crossed, square = carry
    value = 0.5 * (square - jnp.sum(crossed, keepdims=True))
    out_ref[pl.ds(s, 1), :] = jnp.broadcast_to(value, (1, lanes))


def block_energy(theta, pieces):
    n_slot, orbitals, electrons = theta.shape
    vmem = pltpu.MemorySpace.VMEM
    held = sum(p.size * p.dtype.itemsize for p in pieces) + 2 * orbitals * electrons * theta.dtype.itemsize
    out = pl.pallas_call(
        energy_kernel,
        out_shape=jax.ShapeDtypeStruct((n_slot, 128), jnp.float32),
        grid=(n_slot,),
        in_specs=[pl.BlockSpec((1, orbitals, electrons), lambda s: (s, 0, 0))]
        + [pl.BlockSpec(memory_space=vmem)] * len(pieces),
        out_specs=pl.BlockSpec(memory_space=vmem),
        compiler_params=pltpu.CompilerParams(vmem_limit_bytes=int(held + (16 << 20))),
    )(theta, *pieces)
    return out[:, 0]


def swap_pairs(x, axis, size, bit):
    perm = [(i, i ^ bit) for i in range(size)]
    return lax.ppermute(x, axis, perm)


def kick_kernel(source_ref, living_ref, *refs):
    walker_refs = refs[:4]
    field_ref, new_hbm, theta_hbm, walkers, kicked_buf, new_buf, theta_buf, in_sem, out_sem = refs[4:]
    old_dev = walker_refs[0].shape[0]
    n_slot, orbitals, electrons = walkers.shape

    for s in range(n_slot):
        source = source_ref[s]
        for r, walker_ref in enumerate(walker_refs):
            group = source // old_dev
            chosen = group >= r if r == len(walker_refs) - 1 else group == r

            @pl.when(chosen)
            def _(walker_ref=walker_ref, source=source, s=s):
                pltpu.make_async_copy(walker_ref.at[source % old_dev], walkers.at[s], in_sem.at[s]).start()

    scale_all = jnp.transpose(jnp.exp(field_ref[...]))
    rows = lax.broadcasted_iota(jnp.int32, (electrons, electrons), 0)
    cols = lax.broadcasted_iota(jnp.int32, (electrons, electrons), 1)
    eye = rows == cols
    identity = eye.astype(jnp.float32)
    out_copies = []
    intersections = []
    inverses = []
    for s in range(n_slot):
        pltpu.make_async_copy(walker_refs[0].at[0], walkers.at[s], in_sem.at[s]).wait()
        kicked = (scale_all[:, s:s + 1] * walkers[s].astype(jnp.float32)).astype(jnp.bfloat16)
        kicked_buf[s] = kicked
        new_buf[s] = jnp.where(living_ref[s] > 0, kicked, jnp.zeros_like(kicked))
        copy = pltpu.make_async_copy(new_buf.at[s], new_hbm.at[s], out_sem.at[0, s])
        copy.start()
        out_copies.append(copy)
        intersection = kicked[:electrons, :].astype(jnp.float32)
        diagonal = jnp.sum(jnp.where(eye, intersection, 0.0), axis=0, keepdims=True)
        intersections.append(intersection)
        inverses.append(jnp.where(eye, 1.0 / diagonal, 0.0))

    for sweep in range(ITERS):
        products = [
            jnp.dot(x, inv, precision=lax.Precision.HIGHEST, preferred_element_type=jnp.float32)
            for x, inv in zip(intersections, inverses)
        ]
        inverses = [
            jnp.dot(inv, 2.0 * identity - p, precision=lax.Precision.HIGHEST, preferred_element_type=jnp.float32)
            for inv, p in zip(inverses, products)
        ]

    for s in range(n_slot):
        widened = kicked_buf[s].astype(jnp.float32)
        theta = jnp.dot(widened, inverses[s], precision=lax.Precision.HIGHEST, preferred_element_type=jnp.float32)
        theta_buf[s] = theta.astype(jnp.bfloat16)
        copy = pltpu.make_async_copy(theta_buf.at[s], theta_hbm.at[s], out_sem.at[1, s])
        copy.start()
        out_copies.append(copy)
    for copy in out_copies:
        copy.wait()


def kick_operands(old_dev, parent, field, walk_id):
    slot_dev, orbitals = field.shape
    living = (parent >= 0).astype(jnp.int32)
    source = jnp.maximum(parent, 0)
    relative = (source // old_dev) ^ walk_id
    index = (relative * old_dev + source % old_dev).astype(jnp.int32)
    lanes = max(8, -(-slot_dev // 8) * 8)
    padded = jnp.zeros((lanes, orbitals), jnp.float32).at[:slot_dev].set(field)
    return index, living, padded


def kick(old_walkers, beside, across, diagonal_peer, index, living, padded):
    old_dev, orbitals, electrons = old_walkers.shape
    slot_dev = index.shape[0]
    lanes = padded.shape[0]
    any_space = pl.BlockSpec(memory_space=pl.ANY)
    slots = (slot_dev, orbitals, electrons)
    grid_spec = pltpu.PrefetchScalarGridSpec(
        num_scalar_prefetch=2,
        grid=(1,),
        in_specs=[any_space] * 4 + [pl.BlockSpec((lanes, orbitals), lambda i, *_: (0, 0))],
        out_specs=[any_space, any_space],
        scratch_shapes=[
            pltpu.VMEM(slots, jnp.bfloat16),
            pltpu.VMEM(slots, jnp.bfloat16),
            pltpu.VMEM(slots, jnp.bfloat16),
            pltpu.VMEM(slots, jnp.bfloat16),
            pltpu.SemaphoreType.DMA((slot_dev,)),
            pltpu.SemaphoreType.DMA((2, slot_dev)),
        ],
    )
    shape = jax.ShapeDtypeStruct(slots, jnp.bfloat16)
    new_walkers, theta = pl.pallas_call(
        kick_kernel,
        out_shape=[shape, shape],
        grid_spec=grid_spec,
    )(index, living, old_walkers, beside, across, diagonal_peer, padded)
    return new_walkers, theta


def body(old_walkers, half_chol, parent, field):
    n_walk = lax.axis_size("walk")
    walk_id = lax.axis_index("walk")
    core = walk_id % 2

    across = swap_pairs(old_walkers, "walk", n_walk, 2)
    beside = swap_pairs(old_walkers, "walk", n_walk, 1)

    local_g = half_chol.shape[0]
    half_g = local_g // 2
    mine = lax.dynamic_slice_in_dim(half_chol, core * half_g, half_g, axis=0)
    n_chol = lax.axis_size("chol")
    order = list(range(0, n_chol, 2)) + list(range(n_chol - 1, 0, -2))
    forward = [(order[i], order[(i + 1) % n_chol]) for i in range(n_chol)]
    backward = [(b, a) for a, b in forward]
    n_forward = n_chol // 2
    n_backward = n_chol - 1 - n_forward
    walker_step = max(n_forward - 2, 0)
    pieces = []
    handed = []
    ahead = mine
    behind = mine
    new_walkers = theta = None
    operands = kick_operands(old_walkers.shape[0], parent, field, walk_id)
    for step in range(n_forward):
        ahead = lax.ppermute(ahead, "chol", forward)
        carried = [ahead]
        if step < n_backward:
            behind = lax.ppermute(behind, "chol", backward)
            carried.append(behind)
        if step == walker_step:
            carried += [across, beside]
        if step == 0:
            carried += list(operands)
        if step == n_forward - 1:
            diagonal_peer = swap_pairs(across, "walk", n_walk, 1)
            new_walkers, theta = kick(old_walkers, beside, across, diagonal_peer, *operands)
            carried += [new_walkers, theta]
        carried = list(lax.optimization_barrier(tuple(carried)))
        ahead = carried.pop(0)
        arrived = [ahead]
        if step < n_backward:
            behind = carried.pop(0)
            arrived.append(behind)
        if step == walker_step:
            across, beside = carried.pop(0), carried.pop(0)
        if step == 0:
            operands = [carried.pop(0) for item in operands]
        if step == n_forward - 1:
            new_walkers, theta = carried.pop(0), carried.pop(0)
        for piece in arrived:
            pieces.append(piece)
            handed.append(swap_pairs(piece, "walk", n_walk, 1))
    if theta is None:
        diagonal_peer = swap_pairs(across, "walk", n_walk, 1)
        new_walkers, theta = kick(old_walkers, beside, across, diagonal_peer, *operands)

    living = parent >= 0
    energy = block_energy(theta, [half_chol] + pieces + handed)
    energy = jnp.where(living, energy, 0.0)
    return (new_walkers, energy)


def solution(mesh):
    return jax.shard_map(
        body,
        mesh=mesh,
        in_specs=(
            P(("walk", "chol"), None, None),
            P("chol", None, None),
            P(("walk", "chol")),
            P(("walk", "chol"), None),
        ),
        out_specs=(P(("walk", "chol"), None, None), P(("walk", "chol"))),
        check_vma=False,
    )
```

```python
import jax
import jax.numpy as jnp
from jax import lax
from jax.sharding import PartitionSpec as P
from jax.experimental import pallas as pl
from jax.experimental.pallas import tpu as pltpu

ITERS = 3


def green_half(walkers):
    widened = walkers.astype(jnp.float32)
    electrons = walkers.shape[2]
    intersection = widened[:, :electrons, :]
    identity = jnp.eye(electrons, dtype=jnp.float32)
    diagonal = jnp.diagonal(intersection, axis1=1, axis2=2)
    inverse = identity[None, :, :] / diagonal[:, None, :]
    for sweep in range(ITERS):
        product = jnp.einsum("wij,wjk->wik", intersection, inverse, precision=lax.Precision.HIGHEST)
        inverse = jnp.einsum(
            "wij,wjk->wik",
            inverse,
            2.0 * identity[None, :, :] - product,
            precision=lax.Precision.HIGHEST,
        )
    theta = jnp.einsum("wnk,wkj->wnj", widened, inverse, precision=lax.Precision.HIGHEST)
    return theta.astype(jnp.bfloat16)


def energy_kernel(*refs):
    theta_ref = refs[0]
    chol_refs = refs[1:-3]
    out_ref, crossed_ref, square_ref = refs[-3:]
    n_slot, _, electrons = theta_ref.shape
    lanes = out_ref.shape[1]
    rows = lax.broadcasted_iota(jnp.int32, (electrons, electrons), 0)
    cols = lax.broadcasted_iota(jnp.int32, (electrons, electrons), 1)
    diagonal = rows == cols
    crossed_ref[...] = jnp.zeros(crossed_ref.shape, jnp.float32)
    square_ref[...] = jnp.zeros(square_ref.shape, jnp.float32)
    for chol_ref in chol_refs:
        def per_vector(g, carry, chol_ref=chol_ref):
            vector = chol_ref[g]
            for s in range(n_slot):
                blocks = jnp.dot(vector, theta_ref[s], preferred_element_type=jnp.float32)
                crossed_ref[s] += blocks * blocks.T
                diag = jnp.sum(jnp.where(diagonal, blocks, 0.0), axis=0, keepdims=True)
                trace = jnp.sum(diag, axis=1, keepdims=True)
                square_ref[pl.ds(s, 1), :] += jnp.broadcast_to(trace * trace, (1, lanes))
            return carry

        lax.fori_loop(0, chol_ref.shape[0], per_vector, 0)
    for s in range(n_slot):
        crossed = jnp.sum(crossed_ref[s], keepdims=True)
        out_ref[pl.ds(s, 1), :] = 0.5 * (square_ref[pl.ds(s, 1), :] - jnp.broadcast_to(crossed, (1, lanes)))


def block_energy(theta, pieces):
    n_slot, _, electrons = theta.shape
    vmem = pltpu.MemorySpace.VMEM
    held = sum(p.size * p.dtype.itemsize for p in pieces) + theta.size * theta.dtype.itemsize
    out = pl.pallas_call(
        energy_kernel,
        out_shape=jax.ShapeDtypeStruct((n_slot, 128), jnp.float32),
        in_specs=[pl.BlockSpec(memory_space=vmem)] * (1 + len(pieces)),
        out_specs=pl.BlockSpec(memory_space=vmem),
        scratch_shapes=[
            pltpu.VMEM((n_slot, electrons, electrons), jnp.float32),
            pltpu.VMEM((n_slot, 128), jnp.float32),
        ],
        compiler_params=pltpu.CompilerParams(vmem_limit_bytes=int(held + (16 << 20))),
    )(theta, *pieces)
    return out[:, 0]


def swap_pairs(x, axis, size, bit):
    perm = [(i, i ^ bit) for i in range(size)]
    return lax.ppermute(x, axis, perm)


def kick_kernel(source_ref, living_ref, *refs):
    walker_refs = refs[:4]
    field_ref, new_hbm, theta_out, walkers, kicked_buf, new_buf, in_sem, out_sem = refs[4:]
    old_dev = walker_refs[0].shape[0]
    n_slot, orbitals, electrons = walkers.shape

    for s in range(n_slot):
        source = source_ref[s]
        for r, walker_ref in enumerate(walker_refs):
            group = source // old_dev
            chosen = group >= r if r == len(walker_refs) - 1 else group == r

            @pl.when(chosen)
            def _(walker_ref=walker_ref, source=source, s=s):
                pltpu.make_async_copy(walker_ref.at[source % old_dev], walkers.at[s], in_sem.at[s]).start()

    scale_all = jnp.transpose(jnp.exp(field_ref[...]))
    rows = lax.broadcasted_iota(jnp.int32, (electrons, electrons), 0)
    cols = lax.broadcasted_iota(jnp.int32, (electrons, electrons), 1)
    eye = rows == cols
    identity = eye.astype(jnp.float32)
    out_copies = []
    intersections = []
    inverses = []
    for s in range(n_slot):
        pltpu.make_async_copy(walker_refs[0].at[0], walkers.at[s], in_sem.at[s]).wait()
        kicked = (scale_all[:, s:s + 1] * walkers[s].astype(jnp.float32)).astype(jnp.bfloat16)
        kicked_buf[s] = kicked
        new_buf[s] = jnp.where(living_ref[s] > 0, kicked, jnp.zeros_like(kicked))
        copy = pltpu.make_async_copy(new_buf.at[s], new_hbm.at[s], out_sem.at[0, s])
        copy.start()
        out_copies.append(copy)
        intersection = kicked[:electrons, :].astype(jnp.float32)
        diagonal = jnp.sum(jnp.where(eye, intersection, 0.0), axis=0, keepdims=True)
        intersections.append(intersection)
        inverses.append(jnp.where(eye, 1.0 / diagonal, 0.0))

    for sweep in range(ITERS):
        products = [
            jnp.dot(x, inv, precision=lax.Precision.HIGHEST, preferred_element_type=jnp.float32)
            for x, inv in zip(intersections, inverses)
        ]
        inverses = [
            jnp.dot(inv, 2.0 * identity - p, precision=lax.Precision.HIGHEST, preferred_element_type=jnp.float32)
            for inv, p in zip(inverses, products)
        ]

    for s in range(n_slot):
        widened = kicked_buf[s].astype(jnp.float32)
        theta = jnp.dot(widened, inverses[s], precision=lax.Precision.HIGHEST, preferred_element_type=jnp.float32)
        theta_out[s] = theta.astype(jnp.bfloat16)
    for copy in out_copies:
        copy.wait()


def kick_operands(old_dev, parent, field, walk_id):
    slot_dev, orbitals = field.shape
    living = (parent >= 0).astype(jnp.int32)
    source = jnp.maximum(parent, 0)
    relative = (source // old_dev) ^ walk_id
    index = (relative * old_dev + source % old_dev).astype(jnp.int32)
    lanes = max(8, -(-slot_dev // 8) * 8)
    padded = jnp.zeros((lanes, orbitals), jnp.float32).at[:slot_dev].set(field)
    return index, living, padded


def kick(old_walkers, beside, across, diagonal_peer, index, living, padded):
    old_dev, orbitals, electrons = old_walkers.shape
    slot_dev = index.shape[0]
    lanes = padded.shape[0]
    any_space = pl.BlockSpec(memory_space=pl.ANY)
    slots = (slot_dev, orbitals, electrons)
    grid_spec = pltpu.PrefetchScalarGridSpec(
        num_scalar_prefetch=2,
        grid=(1,),
        in_specs=[any_space] * 4 + [pl.BlockSpec((lanes, orbitals), lambda i, *_: (0, 0))],
        out_specs=[any_space, pl.BlockSpec(memory_space=pltpu.MemorySpace.VMEM)],
        scratch_shapes=[
            pltpu.VMEM(slots, jnp.bfloat16),
            pltpu.VMEM(slots, jnp.bfloat16),
            pltpu.VMEM(slots, jnp.bfloat16),
            pltpu.SemaphoreType.DMA((slot_dev,)),
            pltpu.SemaphoreType.DMA((1, slot_dev)),
        ],
    )
    shape = jax.ShapeDtypeStruct(slots, jnp.bfloat16)
    new_walkers, theta = pl.pallas_call(
        kick_kernel,
        out_shape=[shape, shape],
        grid_spec=grid_spec,
    )(index, living, old_walkers, beside, across, diagonal_peer, padded)
    return new_walkers, theta


def body(old_walkers, half_chol, parent, field):
    n_walk = lax.axis_size("walk")
    walk_id = lax.axis_index("walk")
    core = walk_id % 2

    across = swap_pairs(old_walkers, "walk", n_walk, 2)
    beside = swap_pairs(old_walkers, "walk", n_walk, 1)

    local_g = half_chol.shape[0]
    half_g = local_g // 2
    mine = lax.dynamic_slice_in_dim(half_chol, core * half_g, half_g, axis=0)
    n_chol = lax.axis_size("chol")
    order = list(range(0, n_chol, 2)) + list(range(n_chol - 1, 0, -2))
    forward = [(order[i], order[(i + 1) % n_chol]) for i in range(n_chol)]
    backward = [(b, a) for a, b in forward]
    n_forward = n_chol // 2
    n_backward = n_chol - 1 - n_forward
    walker_step = max(n_forward - 2, 0)
    pieces = []
    handed = []
    ahead = mine
    behind = mine
    new_walkers = theta = None
    operands = kick_operands(old_walkers.shape[0], parent, field, walk_id)
    for step in range(n_forward):
        ahead = lax.ppermute(ahead, "chol", forward)
        carried = [ahead]
        if step < n_backward:
            behind = lax.ppermute(behind, "chol", backward)
            carried.append(behind)
        if step == walker_step:
            carried += [across, beside]
        if step == 0:
            carried += list(operands)
        if step == n_forward - 1:
            diagonal_peer = swap_pairs(across, "walk", n_walk, 1)
            new_walkers, theta = kick(old_walkers, beside, across, diagonal_peer, *operands)
            carried += [new_walkers, theta]
        carried = list(lax.optimization_barrier(tuple(carried)))
        ahead = carried.pop(0)
        arrived = [ahead]
        if step < n_backward:
            behind = carried.pop(0)
            arrived.append(behind)
        if step == walker_step:
            across, beside = carried.pop(0), carried.pop(0)
        if step == 0:
            operands = [carried.pop(0) for item in operands]
        if step == n_forward - 1:
            new_walkers, theta = carried.pop(0), carried.pop(0)
        for piece in arrived:
            pieces.append(piece)
            handed.append(swap_pairs(piece, "walk", n_walk, 1))
    if theta is None:
        diagonal_peer = swap_pairs(across, "walk", n_walk, 1)
        new_walkers, theta = kick(old_walkers, beside, across, diagonal_peer, *operands)

    living = parent >= 0
    energy = block_energy(theta, [half_chol] + pieces + handed)
    energy = jnp.where(living, energy, 0.0)
    return (new_walkers, energy)


def solution(mesh):
    return jax.shard_map(
        body,
        mesh=mesh,
        in_specs=(
            P(("walk", "chol"), None, None),
            P("chol", None, None),
            P(("walk", "chol")),
            P(("walk", "chol"), None),
        ),
        out_specs=(P(("walk", "chol"), None, None), P(("walk", "chol"))),
        check_vma=False,
    )
```

```python
import jax
import jax.numpy as jnp
from jax import lax
from jax.sharding import PartitionSpec as P
from jax.experimental import pallas as pl
from jax.experimental.pallas import tpu as pltpu

ITERS = 3


def green_half(walkers):
    widened = walkers.astype(jnp.float32)
    electrons = walkers.shape[2]
    intersection = widened[:, :electrons, :]
    identity = jnp.eye(electrons, dtype=jnp.float32)
    diagonal = jnp.diagonal(intersection, axis1=1, axis2=2)
    inverse = identity[None, :, :] / diagonal[:, None, :]
    for sweep in range(ITERS):
        product = jnp.einsum("wij,wjk->wik", intersection, inverse, precision=lax.Precision.HIGHEST)
        inverse = jnp.einsum(
            "wij,wjk->wik",
            inverse,
            2.0 * identity[None, :, :] - product,
            precision=lax.Precision.HIGHEST,
        )
    theta = jnp.einsum("wnk,wkj->wnj", widened, inverse, precision=lax.Precision.HIGHEST)
    return theta.astype(jnp.bfloat16)


def energy_kernel(*refs):
    theta_ref = refs[0]
    chol_refs = refs[1:-3]
    out_ref, crossed_ref, square_ref = refs[-3:]
    n_slot, _, electrons = theta_ref.shape
    lanes = out_ref.shape[1]
    rows = lax.broadcasted_iota(jnp.int32, (electrons, electrons), 0)
    cols = lax.broadcasted_iota(jnp.int32, (electrons, electrons), 1)
    diagonal = rows == cols
    crossed_ref[...] = jnp.zeros(crossed_ref.shape, jnp.float32)
    square_ref[...] = jnp.zeros(square_ref.shape, jnp.float32)
    for chol_ref in chol_refs:
        def per_vector(g, carry, chol_ref=chol_ref):
            vector = chol_ref[g]
            for s in range(n_slot):
                blocks = jnp.dot(vector, theta_ref[s], preferred_element_type=jnp.float32)
                crossed_ref[s] += blocks * blocks.T
                diag = jnp.sum(jnp.where(diagonal, blocks, 0.0), axis=0, keepdims=True)
                trace = jnp.sum(diag, axis=1, keepdims=True)
                square_ref[pl.ds(s, 1), :] += jnp.broadcast_to(trace * trace, (1, lanes))
            return carry

        lax.fori_loop(0, chol_ref.shape[0], per_vector, 0)
    for s in range(n_slot):
        crossed = jnp.sum(crossed_ref[s], keepdims=True)
        out_ref[pl.ds(s, 1), :] = 0.5 * (square_ref[pl.ds(s, 1), :] - jnp.broadcast_to(crossed, (1, lanes)))


def block_energy(theta, pieces):
    n_slot, _, electrons = theta.shape
    vmem = pltpu.MemorySpace.VMEM
    held = sum(p.size * p.dtype.itemsize for p in pieces) + theta.size * theta.dtype.itemsize
    out = pl.pallas_call(
        energy_kernel,
        out_shape=jax.ShapeDtypeStruct((n_slot, 128), jnp.float32),
        in_specs=[pl.BlockSpec(memory_space=vmem)] * (1 + len(pieces)),
        out_specs=pl.BlockSpec(memory_space=vmem),
        scratch_shapes=[
            pltpu.VMEM((n_slot, electrons, electrons), jnp.float32),
            pltpu.VMEM((n_slot, 128), jnp.float32),
        ],
        compiler_params=pltpu.CompilerParams(vmem_limit_bytes=int(held + (16 << 20))),
    )(theta, *pieces)
    return out[:, 0]


def swap_pairs(x, axis, size, bit):
    perm = [(i, i ^ bit) for i in range(size)]
    return lax.ppermute(x, axis, perm)


def kick_kernel(source_ref, living_ref, *refs):
    walker_refs = refs[:4]
    field_ref, new_hbm, theta_out, walkers, kicked_buf, new_buf, in_sem, out_sem = refs[4:]
    old_dev = walker_refs[0].shape[0]
    n_slot, orbitals, electrons = walkers.shape

    for s in range(n_slot):
        source = source_ref[s]
        for r, walker_ref in enumerate(walker_refs):
            group = source // old_dev
            chosen = group >= r if r == len(walker_refs) - 1 else group == r

            @pl.when(chosen)
            def _(walker_ref=walker_ref, source=source, s=s):
                pltpu.make_async_copy(walker_ref.at[source % old_dev], walkers.at[s], in_sem.at[s]).start()

    scale_all = jnp.transpose(jnp.exp(field_ref[...]))
    rows = lax.broadcasted_iota(jnp.int32, (electrons, electrons), 0)
    cols = lax.broadcasted_iota(jnp.int32, (electrons, electrons), 1)
    eye = rows == cols
    identity = eye.astype(jnp.float32)
    out_copies = []
    intersections = []
    inverses = []
    for s in range(n_slot):
        pltpu.make_async_copy(walker_refs[0].at[0], walkers.at[s], in_sem.at[s]).wait()
        kicked = (scale_all[:, s:s + 1] * walkers[s].astype(jnp.float32)).astype(jnp.bfloat16)
        kicked_buf[s] = kicked
        new_buf[s] = jnp.where(living_ref[s] > 0, kicked, jnp.zeros_like(kicked))
        copy = pltpu.make_async_copy(new_buf.at[s], new_hbm.at[s], out_sem.at[0, s])
        copy.start()
        out_copies.append(copy)
        intersection = kicked[:electrons, :].astype(jnp.float32)
        diagonal = jnp.sum(jnp.where(eye, intersection, 0.0), axis=0, keepdims=True)
        intersections.append(intersection)
        inverses.append(jnp.where(eye, 1.0 / diagonal, 0.0))

    for sweep in range(ITERS):
        products = [
            jnp.dot(x, inv, precision=lax.Precision.HIGHEST, preferred_element_type=jnp.float32)
            for x, inv in zip(intersections, inverses)
        ]
        inverses = [
            jnp.dot(inv, 2.0 * identity - p, precision=lax.Precision.HIGHEST, preferred_element_type=jnp.float32)
            for inv, p in zip(inverses, products)
        ]

    for s in range(n_slot):
        widened = kicked_buf[s].astype(jnp.float32)
        theta = jnp.dot(widened, inverses[s], precision=lax.Precision.HIGHEST, preferred_element_type=jnp.float32)
        theta_out[s] = theta.astype(jnp.bfloat16)
    for copy in out_copies:
        copy.wait()


def kick_operands(old_dev, parent, field, walk_id):
    slot_dev, orbitals = field.shape
    living = (parent >= 0).astype(jnp.int32)
    source = jnp.maximum(parent, 0)
    relative = (source // old_dev) ^ walk_id
    index = (relative * old_dev + source % old_dev).astype(jnp.int32)
    lanes = max(8, -(-slot_dev // 8) * 8)
    padded = jnp.zeros((lanes, orbitals), jnp.float32).at[:slot_dev].set(field)
    return index, living, padded


def kick(old_walkers, beside, across, diagonal_peer, index, living, padded):
    old_dev, orbitals, electrons = old_walkers.shape
    slot_dev = index.shape[0]
    lanes = padded.shape[0]
    any_space = pl.BlockSpec(memory_space=pl.ANY)
    slots = (slot_dev, orbitals, electrons)
    grid_spec = pltpu.PrefetchScalarGridSpec(
        num_scalar_prefetch=2,
        grid=(1,),
        in_specs=[any_space] * 4 + [pl.BlockSpec((lanes, orbitals), lambda i, *_: (0, 0))],
        out_specs=[any_space, pl.BlockSpec(memory_space=pltpu.MemorySpace.VMEM)],
        scratch_shapes=[
            pltpu.VMEM(slots, jnp.bfloat16),
            pltpu.VMEM(slots, jnp.bfloat16),
            pltpu.VMEM(slots, jnp.bfloat16),
            pltpu.SemaphoreType.DMA((slot_dev,)),
            pltpu.SemaphoreType.DMA((1, slot_dev)),
        ],
    )
    shape = jax.ShapeDtypeStruct(slots, jnp.bfloat16)
    new_walkers, theta = pl.pallas_call(
        kick_kernel,
        out_shape=[shape, shape],
        grid_spec=grid_spec,
    )(index, living, old_walkers, beside, across, diagonal_peer, padded)
    return new_walkers, theta


def body(old_walkers, half_chol, parent, field):
    n_walk = lax.axis_size("walk")
    walk_id = lax.axis_index("walk")
    core = walk_id % 2

    across = swap_pairs(old_walkers, "walk", n_walk, 2)
    beside = swap_pairs(old_walkers, "walk", n_walk, 1)

    local_g = half_chol.shape[0]
    half_g = local_g // 2
    mine = lax.dynamic_slice_in_dim(half_chol, core * half_g, half_g, axis=0)
    n_chol = lax.axis_size("chol")
    order = list(range(0, n_chol, 2)) + list(range(n_chol - 1, 0, -2))
    forward = [(order[i], order[(i + 1) % n_chol]) for i in range(n_chol)]
    backward = [(b, a) for a, b in forward]
    n_forward = n_chol // 2
    n_backward = n_chol - 1 - n_forward
    walker_step = max(n_forward - 2, 0)
    pieces = []
    handed = []
    ahead = mine
    behind = mine
    new_walkers = theta = None
    operands = kick_operands(old_walkers.shape[0], parent, field, walk_id)
    for step in range(n_forward):
        ahead = lax.ppermute(ahead, "chol", forward)
        carried = [ahead]
        if step < n_backward:
            behind = lax.ppermute(behind, "chol", backward)
            carried.append(behind)
        if step == walker_step:
            carried += [across, beside]
        if step == 0:
            carried += list(operands)
        if step == n_forward - 1:
            diagonal_peer = swap_pairs(across, "walk", n_walk, 1)
            new_walkers, theta = kick(old_walkers, beside, across, diagonal_peer, *operands)
            carried += [new_walkers, theta]
        carried = list(lax.optimization_barrier(tuple(carried)))
        ahead = carried.pop(0)
        arrived = [ahead]
        if step < n_backward:
            behind = carried.pop(0)
            arrived.append(behind)
        if step == walker_step:
            across, beside = carried.pop(0), carried.pop(0)
        if step == 0:
            operands = [carried.pop(0) for item in operands]
        if step == n_forward - 1:
            new_walkers, theta = carried.pop(0), carried.pop(0)
        for piece in arrived:
            pieces.append(piece)
            handed.append(swap_pairs(piece, "walk", n_walk, 1))
    if theta is None:
        diagonal_peer = swap_pairs(across, "walk", n_walk, 1)
        new_walkers, theta = kick(old_walkers, beside, across, diagonal_peer, *operands)

    living = parent >= 0
    late = 1 if n_forward > n_backward else 2
    energy = block_energy(theta, [half_chol] + pieces[:-late] + handed[:-late])
    energy = energy + block_energy(theta, pieces[-late:] + handed[-late:])
    energy = jnp.where(living, energy, 0.0)
    return (new_walkers, energy)


def solution(mesh):
    return jax.shard_map(
        body,
        mesh=mesh,
        in_specs=(
            P(("walk", "chol"), None, None),
            P("chol", None, None),
            P(("walk", "chol")),
            P(("walk", "chol"), None),
        ),
        out_specs=(P(("walk", "chol"), None, None), P(("walk", "chol"))),
        check_vma=False,
    )
```

```python
import jax
import jax.numpy as jnp
from jax import lax
from jax.sharding import PartitionSpec as P
from jax.experimental import pallas as pl
from jax.experimental.pallas import tpu as pltpu

ITERS = 3


def green_half(walkers):
    widened = walkers.astype(jnp.float32)
    electrons = walkers.shape[2]
    intersection = widened[:, :electrons, :]
    identity = jnp.eye(electrons, dtype=jnp.float32)
    diagonal = jnp.diagonal(intersection, axis1=1, axis2=2)
    inverse = identity[None, :, :] / diagonal[:, None, :]
    for sweep in range(ITERS):
        product = jnp.einsum("wij,wjk->wik", intersection, inverse, precision=lax.Precision.HIGHEST)
        inverse = jnp.einsum(
            "wij,wjk->wik",
            inverse,
            2.0 * identity[None, :, :] - product,
            precision=lax.Precision.HIGHEST,
        )
    theta = jnp.einsum("wnk,wkj->wnj", widened, inverse, precision=lax.Precision.HIGHEST)
    return theta.astype(jnp.bfloat16)


def energy_kernel(*refs):
    theta_ref = refs[0]
    chol_refs = refs[1:-3]
    out_ref, crossed_ref, trace_ref = refs[-3:]
    n_slot, _, electrons = theta_ref.shape
    lanes = out_ref.shape[1]
    rows = lax.broadcasted_iota(jnp.int32, (electrons, electrons), 0)
    cols = lax.broadcasted_iota(jnp.int32, (electrons, electrons), 1)
    diagonal = rows == cols
    crossed_ref[...] = jnp.zeros(crossed_ref.shape, jnp.float32)
    offset = 0
    for chol_ref in chol_refs:
        def per_vector(g, carry, chol_ref=chol_ref, offset=offset):
            vector = chol_ref[g]
            for s in range(n_slot):
                blocks = jnp.dot(vector, theta_ref[s], preferred_element_type=jnp.float32)
                crossed_ref[s] += blocks * blocks.T
                trace_ref[s, pl.ds(offset + g, 1), :] = jnp.sum(jnp.where(diagonal, blocks, 0.0), axis=0, keepdims=True)
            return carry

        lax.fori_loop(0, chol_ref.shape[0], per_vector, 0)
        offset += chol_ref.shape[0]
    for s in range(n_slot):
        traces = jnp.sum(trace_ref[s], axis=1, keepdims=True)
        square = jnp.sum(traces * traces, keepdims=True)
        crossed = jnp.sum(crossed_ref[s], keepdims=True)
        out_ref[pl.ds(s, 1), :] = jnp.broadcast_to(0.5 * (square - crossed), (1, lanes))


def block_energy(theta, pieces):
    n_slot, _, electrons = theta.shape
    n_vectors = sum(p.shape[0] for p in pieces)
    vmem = pltpu.MemorySpace.VMEM
    held = sum(p.size * p.dtype.itemsize for p in pieces) + theta.size * theta.dtype.itemsize
    out = pl.pallas_call(
        energy_kernel,
        out_shape=jax.ShapeDtypeStruct((n_slot, 128), jnp.float32),
        in_specs=[pl.BlockSpec(memory_space=vmem)] * (1 + len(pieces)),
        out_specs=pl.BlockSpec(memory_space=vmem),
        scratch_shapes=[
            pltpu.VMEM((n_slot, electrons, electrons), jnp.float32),
            pltpu.VMEM((n_slot, n_vectors, electrons), jnp.float32),
        ],
        compiler_params=pltpu.CompilerParams(vmem_limit_bytes=int(held + (16 << 20))),
    )(theta, *pieces)
    return out[:, 0]


def swap_pairs(x, axis, size, bit):
    perm = [(i, i ^ bit) for i in range(size)]
    return lax.ppermute(x, axis, perm)


def kick_kernel(source_ref, living_ref, *refs):
    walker_refs = refs[:4]
    field_ref, new_hbm, theta_hbm, walkers, kicked_buf, new_buf, theta_buf, in_sem, out_sem = refs[4:]
    old_dev = walker_refs[0].shape[0]
    n_slot, orbitals, electrons = walkers.shape

    for s in range(n_slot):
        source = source_ref[s]
        for r, walker_ref in enumerate(walker_refs):
            group = source // old_dev
            chosen = group >= r if r == len(walker_refs) - 1 else group == r

            @pl.when(chosen)
            def _(walker_ref=walker_ref, source=source, s=s):
                pltpu.make_async_copy(walker_ref.at[source % old_dev], walkers.at[s], in_sem.at[s]).start()

    scale_all = jnp.transpose(jnp.exp(field_ref[...]))
    rows = lax.broadcasted_iota(jnp.int32, (electrons, electrons), 0)
    cols = lax.broadcasted_iota(jnp.int32, (electrons, electrons), 1)
    eye = rows == cols
    identity = eye.astype(jnp.float32)
    out_copies = []
    intersections = []
    inverses = []
    for s in range(n_slot):
        pltpu.make_async_copy(walker_refs[0].at[0], walkers.at[s], in_sem.at[s]).wait()
        kicked = (scale_all[:, s:s + 1] * walkers[s].astype(jnp.float32)).astype(jnp.bfloat16)
        kicked_buf[s] = kicked
        new_buf[s] = jnp.where(living_ref[s] > 0, kicked, jnp.zeros_like(kicked))
        copy = pltpu.make_async_copy(new_buf.at[s], new_hbm.at[s], out_sem.at[0, s])
        copy.start()
        out_copies.append(copy)
        intersection = kicked[:electrons, :].astype(jnp.float32)
        diagonal = jnp.sum(jnp.where(eye, intersection, 0.0), axis=0, keepdims=True)
        intersections.append(intersection)
        inverses.append(jnp.where(eye, 1.0 / diagonal, 0.0))

    for sweep in range(ITERS):
        products = [
            jnp.dot(x, inv, precision=lax.Precision.HIGHEST, preferred_element_type=jnp.float32)
            for x, inv in zip(intersections, inverses)
        ]
        inverses = [
            jnp.dot(inv, 2.0 * identity - p, precision=lax.Precision.HIGHEST, preferred_element_type=jnp.float32)
            for inv, p in zip(inverses, products)
        ]

    for s in range(n_slot):
        widened = kicked_buf[s].astype(jnp.float32)
        theta = jnp.dot(widened, inverses[s], precision=lax.Precision.HIGHEST, preferred_element_type=jnp.float32)
        theta_buf[s] = theta.astype(jnp.bfloat16)
        copy = pltpu.make_async_copy(theta_buf.at[s], theta_hbm.at[s], out_sem.at[1, s])
        copy.start()
        out_copies.append(copy)
    for copy in out_copies:
        copy.wait()


def kick_operands(old_dev, parent, field, walk_id):
    slot_dev, orbitals = field.shape
    living = (parent >= 0).astype(jnp.int32)
    source = jnp.maximum(parent, 0)
    relative = (source // old_dev) ^ walk_id
    index = (relative * old_dev + source % old_dev).astype(jnp.int32)
    lanes = max(8, -(-slot_dev // 8) * 8)
    padded = jnp.zeros((lanes, orbitals), jnp.float32).at[:slot_dev].set(field)
    return index, living, padded


def kick(old_walkers, beside, across, diagonal_peer, index, living, padded):
    old_dev, orbitals, electrons = old_walkers.shape
    slot_dev = index.shape[0]
    lanes = padded.shape[0]
    any_space = pl.BlockSpec(memory_space=pl.ANY)
    slots = (slot_dev, orbitals, electrons)
    grid_spec = pltpu.PrefetchScalarGridSpec(
        num_scalar_prefetch=2,
        grid=(1,),
        in_specs=[any_space] * 4 + [pl.BlockSpec((lanes, orbitals), lambda i, *_: (0, 0))],
        out_specs=[any_space, any_space],
        scratch_shapes=[
            pltpu.VMEM(slots, jnp.bfloat16),
            pltpu.VMEM(slots, jnp.bfloat16),
            pltpu.VMEM(slots, jnp.bfloat16),
            pltpu.VMEM(slots, jnp.bfloat16),
            pltpu.SemaphoreType.DMA((slot_dev,)),
            pltpu.SemaphoreType.DMA((2, slot_dev)),
        ],
    )
    shape = jax.ShapeDtypeStruct(slots, jnp.bfloat16)
    new_walkers, theta = pl.pallas_call(
        kick_kernel,
        out_shape=[shape, shape],
        grid_spec=grid_spec,
    )(index, living, old_walkers, beside, across, diagonal_peer, padded)
    return new_walkers, theta


def body(old_walkers, half_chol, parent, field):
    n_walk = lax.axis_size("walk")
    walk_id = lax.axis_index("walk")
    core = walk_id % 2

    across = swap_pairs(old_walkers, "walk", n_walk, 2)
    beside = swap_pairs(old_walkers, "walk", n_walk, 1)

    local_g = half_chol.shape[0]
    half_g = local_g // 2
    mine = lax.dynamic_slice_in_dim(half_chol, core * half_g, half_g, axis=0)
    n_chol = lax.axis_size("chol")
    order = list(range(0, n_chol, 2)) + list(range(n_chol - 1, 0, -2))
    forward = [(order[i], order[(i + 1) % n_chol]) for i in range(n_chol)]
    backward = [(b, a) for a, b in forward]
    n_forward = n_chol // 2
    n_backward = n_chol - 1 - n_forward
    walker_step = max(n_forward - 2, 0)
    pieces = []
    handed = []
    ahead = mine
    behind = mine
    new_walkers = theta = None
    operands = kick_operands(old_walkers.shape[0], parent, field, walk_id)
    for step in range(n_forward):
        ahead = lax.ppermute(ahead, "chol", forward)
        carried = [ahead]
        if step < n_backward:
            behind = lax.ppermute(behind, "chol", backward)
            carried.append(behind)
        if step == walker_step:
            carried += [across, beside]
        if step == 0:
            carried += list(operands)
        if step == n_forward - 1:
            diagonal_peer = swap_pairs(across, "walk", n_walk, 1)
            new_walkers, theta = kick(old_walkers, beside, across, diagonal_peer, *operands)
            carried += [new_walkers, theta]
        carried = list(lax.optimization_barrier(tuple(carried)))
        ahead = carried.pop(0)
        arrived = [ahead]
        if step < n_backward:
            behind = carried.pop(0)
            arrived.append(behind)
        if step == walker_step:
            across, beside = carried.pop(0), carried.pop(0)
        if step == 0:
            operands = [carried.pop(0) for item in operands]
        if step == n_forward - 1:
            new_walkers, theta = carried.pop(0), carried.pop(0)
        for piece in arrived:
            pieces.append(piece)
            handed.append(swap_pairs(piece, "walk", n_walk, 1))
    if theta is None:
        diagonal_peer = swap_pairs(across, "walk", n_walk, 1)
        new_walkers, theta = kick(old_walkers, beside, across, diagonal_peer, *operands)

    living = parent >= 0
    energy = block_energy(theta, [half_chol] + pieces + handed)
    energy = jnp.where(living, energy, 0.0)
    return (new_walkers, energy)


def solution(mesh):
    return jax.shard_map(
        body,
        mesh=mesh,
        in_specs=(
            P(("walk", "chol"), None, None),
            P("chol", None, None),
            P(("walk", "chol")),
            P(("walk", "chol"), None),
        ),
        out_specs=(P(("walk", "chol"), None, None), P(("walk", "chol"))),
        check_vma=False,
    )
```

```python
import jax
import jax.numpy as jnp
from jax import lax
from jax.sharding import PartitionSpec as P
from jax.experimental import pallas as pl
from jax.experimental.pallas import tpu as pltpu

ITERS = 3


def green_half(walkers):
    widened = walkers.astype(jnp.float32)
    electrons = walkers.shape[2]
    intersection = widened[:, :electrons, :]
    identity = jnp.eye(electrons, dtype=jnp.float32)
    diagonal = jnp.diagonal(intersection, axis1=1, axis2=2)
    inverse = identity[None, :, :] / diagonal[:, None, :]
    for sweep in range(ITERS):
        product = jnp.einsum("wij,wjk->wik", intersection, inverse, precision=lax.Precision.HIGHEST)
        inverse = jnp.einsum(
            "wij,wjk->wik",
            inverse,
            2.0 * identity[None, :, :] - product,
            precision=lax.Precision.HIGHEST,
        )
    theta = jnp.einsum("wnk,wkj->wnj", widened, inverse, precision=lax.Precision.HIGHEST)
    return theta.astype(jnp.bfloat16)


def energy_kernel(*refs):
    theta_ref = refs[0]
    chol_refs = refs[1:-3]
    out_ref, crossed_ref, trace_ref = refs[-3:]
    n_slot, electrons = trace_ref.shape[0], trace_ref.shape[2]
    lanes = out_ref.shape[1]
    rows = lax.broadcasted_iota(jnp.int32, (electrons, electrons), 0)
    cols = lax.broadcasted_iota(jnp.int32, (electrons, electrons), 1)
    diagonal = rows == cols
    crossed_ref[...] = jnp.zeros(crossed_ref.shape, jnp.float32)
    offset = 0
    for chol_ref in chol_refs:
        def per_vector(g, carry, chol_ref=chol_ref, offset=offset):
            wide = jnp.dot(chol_ref[g], theta_ref[...], preferred_element_type=jnp.float32)
            for s in range(n_slot):
                blocks = wide[:, s * electrons:(s + 1) * electrons]
                crossed_ref[s] += blocks * blocks.T
                trace_ref[s, pl.ds(offset + g, 1), :] = jnp.sum(jnp.where(diagonal, blocks, 0.0), axis=0, keepdims=True)
            return carry

        lax.fori_loop(0, chol_ref.shape[0], per_vector, 0)
        offset += chol_ref.shape[0]
    for s in range(n_slot):
        traces = jnp.sum(trace_ref[s], axis=1, keepdims=True)
        square = jnp.sum(traces * traces, keepdims=True)
        crossed = jnp.sum(crossed_ref[s], keepdims=True)
        out_ref[pl.ds(s, 1), :] = jnp.broadcast_to(0.5 * (square - crossed), (1, lanes))


def block_energy(theta, pieces):
    electrons = pieces[0].shape[1]
    n_slot = theta.shape[1] // electrons
    n_vectors = sum(p.shape[0] for p in pieces)
    vmem = pltpu.MemorySpace.VMEM
    held = sum(p.size * p.dtype.itemsize for p in pieces) + theta.size * theta.dtype.itemsize
    out = pl.pallas_call(
        energy_kernel,
        out_shape=jax.ShapeDtypeStruct((n_slot, 128), jnp.float32),
        in_specs=[pl.BlockSpec(memory_space=vmem)] * (1 + len(pieces)),
        out_specs=pl.BlockSpec(memory_space=vmem),
        scratch_shapes=[
            pltpu.VMEM((n_slot, electrons, electrons), jnp.float32),
            pltpu.VMEM((n_slot, n_vectors, electrons), jnp.float32),
        ],
        compiler_params=pltpu.CompilerParams(vmem_limit_bytes=int(held + (16 << 20))),
    )(theta, *pieces)
    return out[:, 0]


def swap_pairs(x, axis, size, bit):
    perm = [(i, i ^ bit) for i in range(size)]
    return lax.ppermute(x, axis, perm)


def kick_kernel(source_ref, living_ref, *refs):
    walker_refs = refs[:4]
    field_ref, new_hbm, theta_out, walkers, kicked_buf, new_buf, in_sem, out_sem = refs[4:]
    old_dev = walker_refs[0].shape[0]
    n_slot, orbitals, electrons = walkers.shape

    for s in range(n_slot):
        source = source_ref[s]
        for r, walker_ref in enumerate(walker_refs):
            group = source // old_dev
            chosen = group >= r if r == len(walker_refs) - 1 else group == r

            @pl.when(chosen)
            def _(walker_ref=walker_ref, source=source, s=s):
                pltpu.make_async_copy(walker_ref.at[source % old_dev], walkers.at[s], in_sem.at[s]).start()

    scale_all = jnp.transpose(jnp.exp(field_ref[...]))
    rows = lax.broadcasted_iota(jnp.int32, (electrons, electrons), 0)
    cols = lax.broadcasted_iota(jnp.int32, (electrons, electrons), 1)
    eye = rows == cols
    identity = eye.astype(jnp.float32)
    out_copies = []
    intersections = []
    inverses = []
    for s in range(n_slot):
        pltpu.make_async_copy(walker_refs[0].at[0], walkers.at[s], in_sem.at[s]).wait()
        kicked = (scale_all[:, s:s + 1] * walkers[s].astype(jnp.float32)).astype(jnp.bfloat16)
        kicked_buf[s] = kicked
        new_buf[s] = jnp.where(living_ref[s] > 0, kicked, jnp.zeros_like(kicked))
        copy = pltpu.make_async_copy(new_buf.at[s], new_hbm.at[s], out_sem.at[0, s])
        copy.start()
        out_copies.append(copy)
        intersection = kicked[:electrons, :].astype(jnp.float32)
        diagonal = jnp.sum(jnp.where(eye, intersection, 0.0), axis=0, keepdims=True)
        intersections.append(intersection)
        inverses.append(jnp.where(eye, 1.0 / diagonal, 0.0))

    for sweep in range(ITERS):
        products = [
            jnp.dot(x, inv, precision=lax.Precision.HIGHEST, preferred_element_type=jnp.float32)
            for x, inv in zip(intersections, inverses)
        ]
        inverses = [
            jnp.dot(inv, 2.0 * identity - p, precision=lax.Precision.HIGHEST, preferred_element_type=jnp.float32)
            for inv, p in zip(inverses, products)
        ]

    for s in range(n_slot):
        widened = kicked_buf[s].astype(jnp.float32)
        theta = jnp.dot(widened, inverses[s], precision=lax.Precision.HIGHEST, preferred_element_type=jnp.float32)
        theta_out[:, s * electrons:(s + 1) * electrons] = theta.astype(jnp.bfloat16)
    for copy in out_copies:
        copy.wait()


def kick_operands(old_dev, parent, field, walk_id):
    slot_dev, orbitals = field.shape
    living = (parent >= 0).astype(jnp.int32)
    source = jnp.maximum(parent, 0)
    relative = (source // old_dev) ^ walk_id
    index = (relative * old_dev + source % old_dev).astype(jnp.int32)
    lanes = max(8, -(-slot_dev // 8) * 8)
    padded = jnp.zeros((lanes, orbitals), jnp.float32).at[:slot_dev].set(field)
    return index, living, padded


def kick(old_walkers, beside, across, diagonal_peer, index, living, padded):
    old_dev, orbitals, electrons = old_walkers.shape
    slot_dev = index.shape[0]
    lanes = padded.shape[0]
    any_space = pl.BlockSpec(memory_space=pl.ANY)
    slots = (slot_dev, orbitals, electrons)
    grid_spec = pltpu.PrefetchScalarGridSpec(
        num_scalar_prefetch=2,
        grid=(1,),
        in_specs=[any_space] * 4 + [pl.BlockSpec((lanes, orbitals), lambda i, *_: (0, 0))],
        out_specs=[any_space, pl.BlockSpec(memory_space=pltpu.MemorySpace.VMEM)],
        scratch_shapes=[
            pltpu.VMEM(slots, jnp.bfloat16),
            pltpu.VMEM(slots, jnp.bfloat16),
            pltpu.VMEM(slots, jnp.bfloat16),
            pltpu.SemaphoreType.DMA((slot_dev,)),
            pltpu.SemaphoreType.DMA((1, slot_dev)),
        ],
    )
    shape = jax.ShapeDtypeStruct(slots, jnp.bfloat16)
    wide = jax.ShapeDtypeStruct((orbitals, slot_dev * electrons), jnp.bfloat16)
    new_walkers, theta = pl.pallas_call(
        kick_kernel,
        out_shape=[shape, wide],
        grid_spec=grid_spec,
    )(index, living, old_walkers, beside, across, diagonal_peer, padded)
    return new_walkers, theta


def body(old_walkers, half_chol, parent, field):
    n_walk = lax.axis_size("walk")
    walk_id = lax.axis_index("walk")
    core = walk_id % 2

    across = swap_pairs(old_walkers, "walk", n_walk, 2)
    beside = swap_pairs(old_walkers, "walk", n_walk, 1)

    local_g = half_chol.shape[0]
    half_g = local_g // 2
    mine = lax.dynamic_slice_in_dim(half_chol, core * half_g, half_g, axis=0)
    n_chol = lax.axis_size("chol")
    order = list(range(0, n_chol, 2)) + list(range(n_chol - 1, 0, -2))
    forward = [(order[i], order[(i + 1) % n_chol]) for i in range(n_chol)]
    backward = [(b, a) for a, b in forward]
    n_forward = n_chol // 2
    n_backward = n_chol - 1 - n_forward
    walker_step = max(n_forward - 2, 0)
    pieces = []
    handed = []
    ahead = mine
    behind = mine
    new_walkers = theta = None
    operands = kick_operands(old_walkers.shape[0], parent, field, walk_id)
    for step in range(n_forward):
        ahead = lax.ppermute(ahead, "chol", forward)
        carried = [ahead]
        if step < n_backward:
            behind = lax.ppermute(behind, "chol", backward)
            carried.append(behind)
        if step == walker_step:
            carried += [across, beside]
        if step == 0:
            carried += list(operands)
        if step == n_forward - 1:
            diagonal_peer = swap_pairs(across, "walk", n_walk, 1)
            new_walkers, theta = kick(old_walkers, beside, across, diagonal_peer, *operands)
            carried += [new_walkers, theta]
        carried = list(lax.optimization_barrier(tuple(carried)))
        ahead = carried.pop(0)
        arrived = [ahead]
        if step < n_backward:
            behind = carried.pop(0)
            arrived.append(behind)
        if step == walker_step:
            across, beside = carried.pop(0), carried.pop(0)
        if step == 0:
            operands = [carried.pop(0) for item in operands]
        if step == n_forward - 1:
            new_walkers, theta = carried.pop(0), carried.pop(0)
        for piece in arrived:
            pieces.append(piece)
            handed.append(swap_pairs(piece, "walk", n_walk, 1))
    if theta is None:
        diagonal_peer = swap_pairs(across, "walk", n_walk, 1)
        new_walkers, theta = kick(old_walkers, beside, across, diagonal_peer, *operands)

    living = parent >= 0
    energy = block_energy(theta, [half_chol] + pieces + handed)
    energy = jnp.where(living, energy, 0.0)
    return (new_walkers, energy)


def solution(mesh):
    return jax.shard_map(
        body,
        mesh=mesh,
        in_specs=(
            P(("walk", "chol"), None, None),
            P("chol", None, None),
            P(("walk", "chol")),
            P(("walk", "chol"), None),
        ),
        out_specs=(P(("walk", "chol"), None, None), P(("walk", "chol"))),
        check_vma=False,
    )
```

```python
import jax
import jax.numpy as jnp
from jax import lax
from jax.sharding import PartitionSpec as P
from jax.experimental import pallas as pl
from jax.experimental.pallas import tpu as pltpu

ITERS = 3


def green_half(walkers):
    widened = walkers.astype(jnp.float32)
    electrons = walkers.shape[2]
    intersection = widened[:, :electrons, :]
    identity = jnp.eye(electrons, dtype=jnp.float32)
    diagonal = jnp.diagonal(intersection, axis1=1, axis2=2)
    inverse = identity[None, :, :] / diagonal[:, None, :]
    for sweep in range(ITERS):
        product = jnp.einsum("wij,wjk->wik", intersection, inverse, precision=lax.Precision.HIGHEST)
        inverse = jnp.einsum(
            "wij,wjk->wik",
            inverse,
            2.0 * identity[None, :, :] - product,
            precision=lax.Precision.HIGHEST,
        )
    theta = jnp.einsum("wnk,wkj->wnj", widened, inverse, precision=lax.Precision.HIGHEST)
    return theta.astype(jnp.bfloat16)


def energy_kernel(*refs):
    theta_ref = refs[0]
    chol_refs = refs[1:-3]
    out_ref, crossed_ref, trace_ref = refs[-3:]
    n_slot, electrons = trace_ref.shape[0], trace_ref.shape[2]
    lanes = out_ref.shape[1]
    rows = lax.broadcasted_iota(jnp.int32, (electrons, electrons), 0)
    cols = lax.broadcasted_iota(jnp.int32, (electrons, electrons), 1)
    diagonal = rows == cols
    crossed_ref[...] = jnp.zeros(crossed_ref.shape, jnp.float32)
    offset = 0
    for chol_ref in chol_refs:
        def per_vector(g, carry, chol_ref=chol_ref, offset=offset):
            wide = jnp.dot(chol_ref[g], theta_ref[...], preferred_element_type=jnp.float32)
            for s in range(n_slot):
                blocks = wide[:, s * electrons:(s + 1) * electrons]
                crossed_ref[s] += blocks * blocks.T
                trace_ref[s, pl.ds(offset + g, 1), :] = jnp.sum(jnp.where(diagonal, blocks, 0.0), axis=0, keepdims=True)
            return carry

        lax.fori_loop(0, chol_ref.shape[0], per_vector, 0)
        offset += chol_ref.shape[0]
    for s in range(n_slot):
        traces = jnp.sum(trace_ref[s], axis=1, keepdims=True)
        square = jnp.sum(traces * traces, keepdims=True)
        crossed = jnp.sum(crossed_ref[s], keepdims=True)
        out_ref[pl.ds(s, 1), :] = jnp.broadcast_to(0.5 * (square - crossed), (1, lanes))


def block_energy(theta, pieces):
    electrons = pieces[0].shape[1]
    n_slot = theta.shape[1] // electrons
    n_vectors = sum(p.shape[0] for p in pieces)
    vmem = pltpu.MemorySpace.VMEM
    held = sum(p.size * p.dtype.itemsize for p in pieces) + theta.size * theta.dtype.itemsize
    out = pl.pallas_call(
        energy_kernel,
        out_shape=jax.ShapeDtypeStruct((n_slot, 128), jnp.float32),
        in_specs=[pl.BlockSpec(memory_space=vmem)] * (1 + len(pieces)),
        out_specs=pl.BlockSpec(memory_space=vmem),
        scratch_shapes=[
            pltpu.VMEM((n_slot, electrons, electrons), jnp.float32),
            pltpu.VMEM((n_slot, n_vectors, electrons), jnp.float32),
        ],
        compiler_params=pltpu.CompilerParams(vmem_limit_bytes=int(held + (16 << 20))),
    )(theta, *pieces)
    return out[:, 0]


def swap_pairs(x, axis, size, bit):
    perm = [(i, i ^ bit) for i in range(size)]
    return lax.ppermute(x, axis, perm)


def kick_kernel(source_ref, living_ref, *refs):
    walker_refs = refs[:4]
    field_ref, new_hbm, theta_out, walkers, kicked_buf, new_buf, in_sem, out_sem = refs[4:]
    old_dev = walker_refs[0].shape[0]
    n_slot, orbitals, electrons = walkers.shape

    for s in range(n_slot):
        source = source_ref[s]
        for r, walker_ref in enumerate(walker_refs):
            group = source // old_dev
            chosen = group >= r if r == len(walker_refs) - 1 else group == r

            @pl.when(chosen)
            def _(walker_ref=walker_ref, source=source, s=s):
                pltpu.make_async_copy(walker_ref.at[source % old_dev], walkers.at[s], in_sem.at[s]).start()

    scale_all = jnp.transpose(jnp.exp(field_ref[...]))
    rows = lax.broadcasted_iota(jnp.int32, (electrons, electrons), 0)
    cols = lax.broadcasted_iota(jnp.int32, (electrons, electrons), 1)
    eye = rows == cols
    identity = eye.astype(jnp.float32)
    out_copies = []
    intersections = []
    inverses = []
    for s in range(n_slot):
        pltpu.make_async_copy(walker_refs[0].at[0], walkers.at[s], in_sem.at[s]).wait()
        kicked = (scale_all[:, s:s + 1] * walkers[s].astype(jnp.float32)).astype(jnp.bfloat16)
        kicked_buf[s] = kicked
        new_buf[s] = jnp.where(living_ref[s] > 0, kicked, jnp.zeros_like(kicked))
        copy = pltpu.make_async_copy(new_buf.at[s], new_hbm.at[s], out_sem.at[0, s])
        copy.start()
        out_copies.append(copy)
        intersection = kicked[:electrons, :].astype(jnp.float32)
        diagonal = jnp.sum(jnp.where(eye, intersection, 0.0), axis=0, keepdims=True)
        intersections.append(intersection)
        inverses.append(jnp.where(eye, 1.0 / diagonal, 0.0))

    for sweep in range(ITERS):
        products = [
            jnp.dot(x, inv, precision=lax.Precision.HIGHEST, preferred_element_type=jnp.float32)
            for x, inv in zip(intersections, inverses)
        ]
        inverses = [
            jnp.dot(inv, 2.0 * identity - p, precision=lax.Precision.HIGHEST, preferred_element_type=jnp.float32)
            for inv, p in zip(inverses, products)
        ]

    for s in range(n_slot):
        kicked = kicked_buf[s]
        high = inverses[s].astype(jnp.bfloat16)
        rest = inverses[s] - high.astype(jnp.float32)
        middle = rest.astype(jnp.bfloat16)
        low = (rest - middle.astype(jnp.float32)).astype(jnp.bfloat16)
        theta = (
            jnp.dot(kicked, high, preferred_element_type=jnp.float32)
            + jnp.dot(kicked, middle, preferred_element_type=jnp.float32)
            + jnp.dot(kicked, low, preferred_element_type=jnp.float32)
        )
        theta_out[:, s * electrons:(s + 1) * electrons] = theta.astype(jnp.bfloat16)
    for copy in out_copies:
        copy.wait()


def kick_operands(old_dev, parent, field, walk_id):
    slot_dev, orbitals = field.shape
    living = (parent >= 0).astype(jnp.int32)
    source = jnp.maximum(parent, 0)
    relative = (source // old_dev) ^ walk_id
    index = (relative * old_dev + source % old_dev).astype(jnp.int32)
    lanes = max(8, -(-slot_dev // 8) * 8)
    padded = jnp.zeros((lanes, orbitals), jnp.float32).at[:slot_dev].set(field)
    return index, living, padded


def kick(old_walkers, beside, across, diagonal_peer, index, living, padded):
    old_dev, orbitals, electrons = old_walkers.shape
    slot_dev = index.shape[0]
    lanes = padded.shape[0]
    any_space = pl.BlockSpec(memory_space=pl.ANY)
    slots = (slot_dev, orbitals, electrons)
    grid_spec = pltpu.PrefetchScalarGridSpec(
        num_scalar_prefetch=2,
        grid=(1,),
        in_specs=[any_space] * 4 + [pl.BlockSpec((lanes, orbitals), lambda i, *_: (0, 0))],
        out_specs=[any_space, pl.BlockSpec(memory_space=pltpu.MemorySpace.VMEM)],
        scratch_shapes=[
            pltpu.VMEM(slots, jnp.bfloat16),
            pltpu.VMEM(slots, jnp.bfloat16),
            pltpu.VMEM(slots, jnp.bfloat16),
            pltpu.SemaphoreType.DMA((slot_dev,)),
            pltpu.SemaphoreType.DMA((1, slot_dev)),
        ],
    )
    shape = jax.ShapeDtypeStruct(slots, jnp.bfloat16)
    wide = jax.ShapeDtypeStruct((orbitals, slot_dev * electrons), jnp.bfloat16)
    new_walkers, theta = pl.pallas_call(
        kick_kernel,
        out_shape=[shape, wide],
        grid_spec=grid_spec,
    )(index, living, old_walkers, beside, across, diagonal_peer, padded)
    return new_walkers, theta


def body(old_walkers, half_chol, parent, field):
    n_walk = lax.axis_size("walk")
    walk_id = lax.axis_index("walk")
    core = walk_id % 2

    across = swap_pairs(old_walkers, "walk", n_walk, 2)
    beside = swap_pairs(old_walkers, "walk", n_walk, 1)

    local_g = half_chol.shape[0]
    half_g = local_g // 2
    mine = lax.dynamic_slice_in_dim(half_chol, core * half_g, half_g, axis=0)
    n_chol = lax.axis_size("chol")
    order = list(range(0, n_chol, 2)) + list(range(n_chol - 1, 0, -2))
    forward = [(order[i], order[(i + 1) % n_chol]) for i in range(n_chol)]
    backward = [(b, a) for a, b in forward]
    n_forward = n_chol // 2
    n_backward = n_chol - 1 - n_forward
    walker_step = max(n_forward - 2, 0)
    pieces = []
    handed = []
    ahead = mine
    behind = mine
    new_walkers = theta = None
    operands = kick_operands(old_walkers.shape[0], parent, field, walk_id)
    for step in range(n_forward):
        ahead = lax.ppermute(ahead, "chol", forward)
        carried = [ahead]
        if step < n_backward:
            behind = lax.ppermute(behind, "chol", backward)
            carried.append(behind)
        if step == walker_step:
            carried += [across, beside]
        if step == 0:
            carried += list(operands)
        if step == n_forward - 1:
            diagonal_peer = swap_pairs(across, "walk", n_walk, 1)
            new_walkers, theta = kick(old_walkers, beside, across, diagonal_peer, *operands)
            carried += [new_walkers, theta]
        carried = list(lax.optimization_barrier(tuple(carried)))
        ahead = carried.pop(0)
        arrived = [ahead]
        if step < n_backward:
            behind = carried.pop(0)
            arrived.append(behind)
        if step == walker_step:
            across, beside = carried.pop(0), carried.pop(0)
        if step == 0:
            operands = [carried.pop(0) for item in operands]
        if step == n_forward - 1:
            new_walkers, theta = carried.pop(0), carried.pop(0)
        for piece in arrived:
            pieces.append(piece)
            handed.append(swap_pairs(piece, "walk", n_walk, 1))
    if theta is None:
        diagonal_peer = swap_pairs(across, "walk", n_walk, 1)
        new_walkers, theta = kick(old_walkers, beside, across, diagonal_peer, *operands)

    living = parent >= 0
    energy = block_energy(theta, [half_chol] + pieces + handed)
    energy = jnp.where(living, energy, 0.0)
    return (new_walkers, energy)


def solution(mesh):
    return jax.shard_map(
        body,
        mesh=mesh,
        in_specs=(
            P(("walk", "chol"), None, None),
            P("chol", None, None),
            P(("walk", "chol")),
            P(("walk", "chol"), None),
        ),
        out_specs=(P(("walk", "chol"), None, None), P(("walk", "chol"))),
        check_vma=False,
    )
```

```python
import jax
import jax.numpy as jnp
from jax import lax
from jax.sharding import PartitionSpec as P
from jax.experimental import pallas as pl
from jax.experimental.pallas import tpu as pltpu

ITERS = 3


def green_half(walkers):
    widened = walkers.astype(jnp.float32)
    electrons = walkers.shape[2]
    intersection = widened[:, :electrons, :]
    identity = jnp.eye(electrons, dtype=jnp.float32)
    diagonal = jnp.diagonal(intersection, axis1=1, axis2=2)
    inverse = identity[None, :, :] / diagonal[:, None, :]
    for sweep in range(ITERS):
        product = jnp.einsum("wij,wjk->wik", intersection, inverse, precision=lax.Precision.HIGHEST)
        inverse = jnp.einsum(
            "wij,wjk->wik",
            inverse,
            2.0 * identity[None, :, :] - product,
            precision=lax.Precision.HIGHEST,
        )
    theta = jnp.einsum("wnk,wkj->wnj", widened, inverse, precision=lax.Precision.HIGHEST)
    return theta.astype(jnp.bfloat16)


def energy_kernel(*refs):
    theta_ref = refs[0]
    chol_refs = refs[1:-3]
    out_ref, crossed_ref, trace_ref = refs[-3:]
    n_slot, electrons = trace_ref.shape[0], trace_ref.shape[2]
    lanes = out_ref.shape[1]
    rows = lax.broadcasted_iota(jnp.int32, (electrons, electrons), 0)
    cols = lax.broadcasted_iota(jnp.int32, (electrons, electrons), 1)
    diagonal = rows == cols
    crossed_ref[...] = jnp.zeros(crossed_ref.shape, jnp.float32)
    offset = 0
    for chol_ref in chol_refs:
        def per_vector(g, carry, chol_ref=chol_ref, offset=offset):
            wide = jnp.dot(chol_ref[g], theta_ref[...], preferred_element_type=jnp.float32)
            for s in range(n_slot):
                blocks = wide[:, s * electrons:(s + 1) * electrons]
                crossed_ref[s] += blocks * blocks.T
                trace_ref[s, pl.ds(offset + g, 1), :] = jnp.sum(jnp.where(diagonal, blocks, 0.0), axis=0, keepdims=True)
            return carry

        lax.fori_loop(0, chol_ref.shape[0], per_vector, 0)
        offset += chol_ref.shape[0]
    for s in range(n_slot):
        traces = jnp.sum(trace_ref[s], axis=1, keepdims=True)
        square = jnp.sum(traces * traces, keepdims=True)
        crossed = jnp.sum(crossed_ref[s], keepdims=True)
        out_ref[pl.ds(s, 1), :] = jnp.broadcast_to(0.5 * (square - crossed), (1, lanes))


def block_energy(theta, pieces):
    electrons = pieces[0].shape[1]
    n_slot = theta.shape[1] // electrons
    n_vectors = sum(p.shape[0] for p in pieces)
    vmem = pltpu.MemorySpace.VMEM
    held = sum(p.size * p.dtype.itemsize for p in pieces) + theta.size * theta.dtype.itemsize
    out = pl.pallas_call(
        energy_kernel,
        out_shape=jax.ShapeDtypeStruct((n_slot, 128), jnp.float32),
        in_specs=[pl.BlockSpec(memory_space=vmem)] * (1 + len(pieces)),
        out_specs=pl.BlockSpec(memory_space=vmem),
        scratch_shapes=[
            pltpu.VMEM((n_slot, electrons, electrons), jnp.float32),
            pltpu.VMEM((n_slot, n_vectors, electrons), jnp.float32),
        ],
        compiler_params=pltpu.CompilerParams(vmem_limit_bytes=int(held + (16 << 20))),
    )(theta, *pieces)
    return out[:, 0]


def swap_pairs(x, axis, size, bit):
    perm = [(i, i ^ bit) for i in range(size)]
    return lax.ppermute(x, axis, perm)


def exact_bf16_product(exact, wide):
    high = wide.astype(jnp.bfloat16)
    rest = wide - high.astype(jnp.float32)
    middle = rest.astype(jnp.bfloat16)
    low = (rest - middle.astype(jnp.float32)).astype(jnp.bfloat16)
    return (
        jnp.dot(exact, high, preferred_element_type=jnp.float32)
        + jnp.dot(exact, middle, preferred_element_type=jnp.float32)
        + jnp.dot(exact, low, preferred_element_type=jnp.float32)
    )


def kick_kernel(source_ref, living_ref, *refs):
    walker_refs = refs[:4]
    field_ref, new_hbm, theta_out, walkers, kicked_buf, new_buf, in_sem, out_sem = refs[4:]
    old_dev = walker_refs[0].shape[0]
    n_slot, orbitals, electrons = walkers.shape

    for s in range(n_slot):
        source = source_ref[s]
        for r, walker_ref in enumerate(walker_refs):
            group = source // old_dev
            chosen = group >= r if r == len(walker_refs) - 1 else group == r

            @pl.when(chosen)
            def _(walker_ref=walker_ref, source=source, s=s):
                pltpu.make_async_copy(walker_ref.at[source % old_dev], walkers.at[s], in_sem.at[s]).start()

    scale_all = jnp.transpose(jnp.exp(field_ref[...]))
    rows = lax.broadcasted_iota(jnp.int32, (electrons, electrons), 0)
    cols = lax.broadcasted_iota(jnp.int32, (electrons, electrons), 1)
    eye = rows == cols
    identity = eye.astype(jnp.float32)
    out_copies = []
    intersections = []
    inverses = []
    for s in range(n_slot):
        pltpu.make_async_copy(walker_refs[0].at[0], walkers.at[s], in_sem.at[s]).wait()
        kicked = (scale_all[:, s:s + 1] * walkers[s].astype(jnp.float32)).astype(jnp.bfloat16)
        kicked_buf[s] = kicked
        new_buf[s] = jnp.where(living_ref[s] > 0, kicked, jnp.zeros_like(kicked))
        copy = pltpu.make_async_copy(new_buf.at[s], new_hbm.at[s], out_sem.at[0, s])
        copy.start()
        out_copies.append(copy)
        intersection = kicked[:electrons, :]
        diagonal = jnp.sum(jnp.where(eye, intersection.astype(jnp.float32), 0.0), axis=0, keepdims=True)
        intersections.append(intersection)
        inverses.append(jnp.where(eye, 1.0 / diagonal, 0.0))

    for sweep in range(ITERS):
        products = [exact_bf16_product(x, inv) for x, inv in zip(intersections, inverses)]
        inverses = [
            jnp.dot(inv, 2.0 * identity - p, precision=lax.Precision.HIGHEST, preferred_element_type=jnp.float32)
            for inv, p in zip(inverses, products)
        ]

    for s in range(n_slot):
        theta = exact_bf16_product(kicked_buf[s], inverses[s])
        theta_out[:, s * electrons:(s + 1) * electrons] = theta.astype(jnp.bfloat16)
    for copy in out_copies:
        copy.wait()


def kick_operands(old_dev, parent, field, walk_id):
    slot_dev, orbitals = field.shape
    living = (parent >= 0).astype(jnp.int32)
    source = jnp.maximum(parent, 0)
    relative = (source // old_dev) ^ walk_id
    index = (relative * old_dev + source % old_dev).astype(jnp.int32)
    lanes = max(8, -(-slot_dev // 8) * 8)
    padded = jnp.zeros((lanes, orbitals), jnp.float32).at[:slot_dev].set(field)
    return index, living, padded


def kick(old_walkers, beside, across, diagonal_peer, index, living, padded):
    old_dev, orbitals, electrons = old_walkers.shape
    slot_dev = index.shape[0]
    lanes = padded.shape[0]
    any_space = pl.BlockSpec(memory_space=pl.ANY)
    slots = (slot_dev, orbitals, electrons)
    grid_spec = pltpu.PrefetchScalarGridSpec(
        num_scalar_prefetch=2,
        grid=(1,),
        in_specs=[any_space] * 4 + [pl.BlockSpec((lanes, orbitals), lambda i, *_: (0, 0))],
        out_specs=[any_space, pl.BlockSpec(memory_space=pltpu.MemorySpace.VMEM)],
        scratch_shapes=[
            pltpu.VMEM(slots, jnp.bfloat16),
            pltpu.VMEM(slots, jnp.bfloat16),
            pltpu.VMEM(slots, jnp.bfloat16),
            pltpu.SemaphoreType.DMA((slot_dev,)),
            pltpu.SemaphoreType.DMA((1, slot_dev)),
        ],
    )
    shape = jax.ShapeDtypeStruct(slots, jnp.bfloat16)
    wide = jax.ShapeDtypeStruct((orbitals, slot_dev * electrons), jnp.bfloat16)
    new_walkers, theta = pl.pallas_call(
        kick_kernel,
        out_shape=[shape, wide],
        grid_spec=grid_spec,
    )(index, living, old_walkers, beside, across, diagonal_peer, padded)
    return new_walkers, theta


def body(old_walkers, half_chol, parent, field):
    n_walk = lax.axis_size("walk")
    walk_id = lax.axis_index("walk")
    core = walk_id % 2

    across = swap_pairs(old_walkers, "walk", n_walk, 2)
    beside = swap_pairs(old_walkers, "walk", n_walk, 1)

    local_g = half_chol.shape[0]
    half_g = local_g // 2
    mine = lax.dynamic_slice_in_dim(half_chol, core * half_g, half_g, axis=0)
    n_chol = lax.axis_size("chol")
    order = list(range(0, n_chol, 2)) + list(range(n_chol - 1, 0, -2))
    forward = [(order[i], order[(i + 1) % n_chol]) for i in range(n_chol)]
    backward = [(b, a) for a, b in forward]
    n_forward = n_chol // 2
    n_backward = n_chol - 1 - n_forward
    walker_step = max(n_forward - 2, 0)
    pieces = []
    handed = []
    ahead = mine
    behind = mine
    new_walkers = theta = None
    operands = kick_operands(old_walkers.shape[0], parent, field, walk_id)
    for step in range(n_forward):
        ahead = lax.ppermute(ahead, "chol", forward)
        carried = [ahead]
        if step < n_backward:
            behind = lax.ppermute(behind, "chol", backward)
            carried.append(behind)
        if step == walker_step:
            carried += [across, beside]
        if step == 0:
            carried += list(operands)
        if step == n_forward - 1:
            diagonal_peer = swap_pairs(across, "walk", n_walk, 1)
            new_walkers, theta = kick(old_walkers, beside, across, diagonal_peer, *operands)
            carried += [new_walkers, theta]
        carried = list(lax.optimization_barrier(tuple(carried)))
        ahead = carried.pop(0)
        arrived = [ahead]
        if step < n_backward:
            behind = carried.pop(0)
            arrived.append(behind)
        if step == walker_step:
            across, beside = carried.pop(0), carried.pop(0)
        if step == 0:
            operands = [carried.pop(0) for item in operands]
        if step == n_forward - 1:
            new_walkers, theta = carried.pop(0), carried.pop(0)
        for piece in arrived:
            pieces.append(piece)
            handed.append(swap_pairs(piece, "walk", n_walk, 1))
    if theta is None:
        diagonal_peer = swap_pairs(across, "walk", n_walk, 1)
        new_walkers, theta = kick(old_walkers, beside, across, diagonal_peer, *operands)

    living = parent >= 0
    energy = block_energy(theta, [half_chol] + pieces + handed)
    energy = jnp.where(living, energy, 0.0)
    return (new_walkers, energy)


def solution(mesh):
    return jax.shard_map(
        body,
        mesh=mesh,
        in_specs=(
            P(("walk", "chol"), None, None),
            P("chol", None, None),
            P(("walk", "chol")),
            P(("walk", "chol"), None),
        ),
        out_specs=(P(("walk", "chol"), None, None), P(("walk", "chol"))),
        check_vma=False,
    )
```

```python
import jax
import jax.numpy as jnp
from jax import lax
from jax.sharding import PartitionSpec as P
from jax.experimental import pallas as pl
from jax.experimental.pallas import tpu as pltpu

ITERS = 3


def green_half(walkers):
    widened = walkers.astype(jnp.float32)
    electrons = walkers.shape[2]
    intersection = widened[:, :electrons, :]
    identity = jnp.eye(electrons, dtype=jnp.float32)
    diagonal = jnp.diagonal(intersection, axis1=1, axis2=2)
    inverse = identity[None, :, :] / diagonal[:, None, :]
    for sweep in range(ITERS):
        product = jnp.einsum("wij,wjk->wik", intersection, inverse, precision=lax.Precision.HIGHEST)
        inverse = jnp.einsum(
            "wij,wjk->wik",
            inverse,
            2.0 * identity[None, :, :] - product,
            precision=lax.Precision.HIGHEST,
        )
    theta = jnp.einsum("wnk,wkj->wnj", widened, inverse, precision=lax.Precision.HIGHEST)
    return theta.astype(jnp.bfloat16)


def energy_kernel(*refs):
    theta_ref = refs[0]
    chol_refs = refs[1:-3]
    out_ref, crossed_ref, trace_ref = refs[-3:]
    n_slot, electrons = trace_ref.shape[0], trace_ref.shape[2]
    lanes = out_ref.shape[1]
    rows = lax.broadcasted_iota(jnp.int32, (electrons, electrons), 0)
    cols = lax.broadcasted_iota(jnp.int32, (electrons, electrons), 1)
    diagonal = rows == cols
    crossed_ref[...] = jnp.zeros(crossed_ref.shape, jnp.float32)
    offset = 0
    for chol_ref in chol_refs:
        def per_vector(g, carry, chol_ref=chol_ref, offset=offset):
            wide = jnp.dot(chol_ref[g], theta_ref[...], preferred_element_type=jnp.float32)
            for s in range(n_slot):
                blocks = wide[:, s * electrons:(s + 1) * electrons]
                crossed_ref[s] += blocks * blocks.T
                trace_ref[s, pl.ds(offset + g, 1), :] = jnp.sum(jnp.where(diagonal, blocks, 0.0), axis=0, keepdims=True)
            return carry

        lax.fori_loop(0, chol_ref.shape[0], per_vector, 0)
        offset += chol_ref.shape[0]
    for s in range(n_slot):
        traces = jnp.sum(trace_ref[s], axis=1, keepdims=True)
        square = jnp.sum(traces * traces, keepdims=True)
        crossed = jnp.sum(crossed_ref[s], keepdims=True)
        out_ref[pl.ds(s, 1), :] = jnp.broadcast_to(0.5 * (square - crossed), (1, lanes))


def block_energy(theta, pieces):
    electrons = pieces[0].shape[1]
    n_slot = theta.shape[1] // electrons
    n_vectors = sum(p.shape[0] for p in pieces)
    vmem = pltpu.MemorySpace.VMEM
    held = sum(p.size * p.dtype.itemsize for p in pieces) + theta.size * theta.dtype.itemsize
    out = pl.pallas_call(
        energy_kernel,
        out_shape=jax.ShapeDtypeStruct((n_slot, 128), jnp.float32),
        in_specs=[pl.BlockSpec(memory_space=vmem)] * (1 + len(pieces)),
        out_specs=pl.BlockSpec(memory_space=vmem),
        scratch_shapes=[
            pltpu.VMEM((n_slot, electrons, electrons), jnp.float32),
            pltpu.VMEM((n_slot, n_vectors, electrons), jnp.float32),
        ],
        compiler_params=pltpu.CompilerParams(vmem_limit_bytes=int(held + (16 << 20))),
    )(theta, *pieces)
    return out[:, 0]


def swap_pairs(x, axis, size, bit):
    perm = [(i, i ^ bit) for i in range(size)]
    return lax.ppermute(x, axis, perm)


def exact_bf16_product(exact, wide):
    high = wide.astype(jnp.bfloat16)
    rest = wide - high.astype(jnp.float32)
    middle = rest.astype(jnp.bfloat16)
    low = (rest - middle.astype(jnp.float32)).astype(jnp.bfloat16)
    return (
        jnp.dot(exact, high, preferred_element_type=jnp.float32)
        + jnp.dot(exact, middle, preferred_element_type=jnp.float32)
        + jnp.dot(exact, low, preferred_element_type=jnp.float32)
    )


def split_product(left, right):
    left_high = left.astype(jnp.bfloat16)
    left_low = (left - left_high.astype(jnp.float32)).astype(jnp.bfloat16)
    right_high = right.astype(jnp.bfloat16)
    right_low = (right - right_high.astype(jnp.float32)).astype(jnp.bfloat16)
    return (
        jnp.dot(left_high, right_high, preferred_element_type=jnp.float32)
        + jnp.dot(left_high, right_low, preferred_element_type=jnp.float32)
        + jnp.dot(left_low, right_high, preferred_element_type=jnp.float32)
    )


def kick_kernel(source_ref, living_ref, *refs):
    walker_refs = refs[:4]
    field_ref, new_hbm, theta_out, walkers, kicked_buf, new_buf, in_sem, out_sem = refs[4:]
    old_dev = walker_refs[0].shape[0]
    n_slot, orbitals, electrons = walkers.shape

    for s in range(n_slot):
        source = source_ref[s]
        for r, walker_ref in enumerate(walker_refs):
            group = source // old_dev
            chosen = group >= r if r == len(walker_refs) - 1 else group == r

            @pl.when(chosen)
            def _(walker_ref=walker_ref, source=source, s=s):
                pltpu.make_async_copy(walker_ref.at[source % old_dev], walkers.at[s], in_sem.at[s]).start()

    scale_all = jnp.transpose(jnp.exp(field_ref[...]))
    rows = lax.broadcasted_iota(jnp.int32, (electrons, electrons), 0)
    cols = lax.broadcasted_iota(jnp.int32, (electrons, electrons), 1)
    eye = rows == cols
    identity = eye.astype(jnp.float32)
    out_copies = []
    intersections = []
    inverses = []
    for s in range(n_slot):
        pltpu.make_async_copy(walker_refs[0].at[0], walkers.at[s], in_sem.at[s]).wait()
        kicked = (scale_all[:, s:s + 1] * walkers[s].astype(jnp.float32)).astype(jnp.bfloat16)
        kicked_buf[s] = kicked
        new_buf[s] = jnp.where(living_ref[s] > 0, kicked, jnp.zeros_like(kicked))
        copy = pltpu.make_async_copy(new_buf.at[s], new_hbm.at[s], out_sem.at[0, s])
        copy.start()
        out_copies.append(copy)
        intersection = kicked[:electrons, :]
        diagonal = jnp.sum(jnp.where(eye, intersection.astype(jnp.float32), 0.0), axis=0, keepdims=True)
        intersections.append(intersection)
        inverses.append(jnp.where(eye, 1.0 / diagonal, 0.0))

    for sweep in range(ITERS):
        products = [exact_bf16_product(x, inv) for x, inv in zip(intersections, inverses)]
        inverses = [split_product(inv, 2.0 * identity - p) for inv, p in zip(inverses, products)]

    for s in range(n_slot):
        theta = exact_bf16_product(kicked_buf[s], inverses[s])
        theta_out[:, s * electrons:(s + 1) * electrons] = theta.astype(jnp.bfloat16)
    for copy in out_copies:
        copy.wait()


def kick_operands(old_dev, parent, field, walk_id):
    slot_dev, orbitals = field.shape
    living = (parent >= 0).astype(jnp.int32)
    source = jnp.maximum(parent, 0)
    relative = (source // old_dev) ^ walk_id
    index = (relative * old_dev + source % old_dev).astype(jnp.int32)
    lanes = max(8, -(-slot_dev // 8) * 8)
    padded = jnp.zeros((lanes, orbitals), jnp.float32).at[:slot_dev].set(field)
    return index, living, padded


def kick(old_walkers, beside, across, diagonal_peer, index, living, padded):
    old_dev, orbitals, electrons = old_walkers.shape
    slot_dev = index.shape[0]
    lanes = padded.shape[0]
    any_space = pl.BlockSpec(memory_space=pl.ANY)
    slots = (slot_dev, orbitals, electrons)
    grid_spec = pltpu.PrefetchScalarGridSpec(
        num_scalar_prefetch=2,
        grid=(1,),
        in_specs=[any_space] * 4 + [pl.BlockSpec((lanes, orbitals), lambda i, *_: (0, 0))],
        out_specs=[any_space, pl.BlockSpec(memory_space=pltpu.MemorySpace.VMEM)],
        scratch_shapes=[
            pltpu.VMEM(slots, jnp.bfloat16),
            pltpu.VMEM(slots, jnp.bfloat16),
            pltpu.VMEM(slots, jnp.bfloat16),
            pltpu.SemaphoreType.DMA((slot_dev,)),
            pltpu.SemaphoreType.DMA((1, slot_dev)),
        ],
    )
    shape = jax.ShapeDtypeStruct(slots, jnp.bfloat16)
    wide = jax.ShapeDtypeStruct((orbitals, slot_dev * electrons), jnp.bfloat16)
    new_walkers, theta = pl.pallas_call(
        kick_kernel,
        out_shape=[shape, wide],
        grid_spec=grid_spec,
    )(index, living, old_walkers, beside, across, diagonal_peer, padded)
    return new_walkers, theta


def body(old_walkers, half_chol, parent, field):
    n_walk = lax.axis_size("walk")
    walk_id = lax.axis_index("walk")
    core = walk_id % 2

    across = swap_pairs(old_walkers, "walk", n_walk, 2)
    beside = swap_pairs(old_walkers, "walk", n_walk, 1)

    local_g = half_chol.shape[0]
    half_g = local_g // 2
    mine = lax.dynamic_slice_in_dim(half_chol, core * half_g, half_g, axis=0)
    n_chol = lax.axis_size("chol")
    order = list(range(0, n_chol, 2)) + list(range(n_chol - 1, 0, -2))
    forward = [(order[i], order[(i + 1) % n_chol]) for i in range(n_chol)]
    backward = [(b, a) for a, b in forward]
    n_forward = n_chol // 2
    n_backward = n_chol - 1 - n_forward
    walker_step = max(n_forward - 2, 0)
    pieces = []
    handed = []
    ahead = mine
    behind = mine
    new_walkers = theta = None
    operands = kick_operands(old_walkers.shape[0], parent, field, walk_id)
    for step in range(n_forward):
        ahead = lax.ppermute(ahead, "chol", forward)
        carried = [ahead]
        if step < n_backward:
            behind = lax.ppermute(behind, "chol", backward)
            carried.append(behind)
        if step == walker_step:
            carried += [across, beside]
        if step == 0:
            carried += list(operands)
        if step == n_forward - 1:
            diagonal_peer = swap_pairs(across, "walk", n_walk, 1)
            new_walkers, theta = kick(old_walkers, beside, across, diagonal_peer, *operands)
            carried += [new_walkers, theta]
        carried = list(lax.optimization_barrier(tuple(carried)))
        ahead = carried.pop(0)
        arrived = [ahead]
        if step < n_backward:
            behind = carried.pop(0)
            arrived.append(behind)
        if step == walker_step:
            across, beside = carried.pop(0), carried.pop(0)
        if step == 0:
            operands = [carried.pop(0) for item in operands]
        if step == n_forward - 1:
            new_walkers, theta = carried.pop(0), carried.pop(0)
        for piece in arrived:
            pieces.append(piece)
            handed.append(swap_pairs(piece, "walk", n_walk, 1))
    if theta is None:
        diagonal_peer = swap_pairs(across, "walk", n_walk, 1)
        new_walkers, theta = kick(old_walkers, beside, across, diagonal_peer, *operands)

    living = parent >= 0
    energy = block_energy(theta, [half_chol] + pieces + handed)
    energy = jnp.where(living, energy, 0.0)
    return (new_walkers, energy)


def solution(mesh):
    return jax.shard_map(
        body,
        mesh=mesh,
        in_specs=(
            P(("walk", "chol"), None, None),
            P("chol", None, None),
            P(("walk", "chol")),
            P(("walk", "chol"), None),
        ),
        out_specs=(P(("walk", "chol"), None, None), P(("walk", "chol"))),
        check_vma=False,
    )
```
